256 devices in a mesh: dp: 16 (over z, core), seq: 16 (over y, x).
Axes of the slice: x: 4, y: 4, z: 8, core: 2. Of those that a mesh axis runs over, the one named last changes fastest.
Arguments:
- clean_frames: bfloat16 [16, 2048, 1024], P('dp', 'seq')
- noise_frames: bfloat16 [16, 2048, 1024], P('dp', 'seq'), may hold values from -6 to 6
- lengths: int32 [16], P('dp'), may hold values from 512 to 2048
- group_ids: int32 [16, 2048], P('dp'), may hold values from 0 to 255, never falling along the last dimension, each value on 1 to 25 neighbouring positions
- time_index: int32 [16], P('dp'), may hold values from 0 to 999
- modulation: float32 [1024], replicated, may hold values from -4 to 4
- teacher_qkv: bfloat16 [1024, 3072], replicated, may hold values from -0.1875 to 0.1875
- teacher_out: bfloat16 [1024, 1024], replicated, may hold values from -6 to 6
- student_in: bfloat16 [3, 1024, 1024], P(None, ('dp', 'seq')), may hold values from -0.1875 to 0.1875
- student_out: bfloat16 [1024, 1024], P(('dp', 'seq')), may hold values from -1 to 1
Outputs:
- grad_inputs: float32 [2, 1024, 1024], P(None, ('dp', 'seq'))
- mean_error: float32 [], replicated
The draws below stay inside these ranges and needn't reach their ends.
Inputs may be any that keep to these rules, and one draw needn't show every extreme that they name: `group_ids`: group numbers never fall along a dialogue, and each group holds 1 to 25 frames.
All inputs are finite; a program needn't handle non-finite values.
Results may differ from the reference program's by a relative error of at most 0.015.
Values may be sent and summed in bfloat16 or wider, within the bound.
No kernel may reach another device: no remote copies, remote signals or barrier semaphores. Data moves between devices by JAX's collectives and lax.ppermute only.
A program may use at most 128 MiB of HBM per device.

```python
import math
import jax
import jax.numpy as jnp
import numpy as np
from jax import lax

D = 1024
HEADS = 16
FR_DEV = 128
GROUP = 25
HALO = 64
TSTEPS = 1000
FRAMES = 2048
BATCH = 16
NCHUNK = 256
N_SEQ = 16


def draw_clean_frames(key, part):
    base = jax.random.normal(key, (BATCH, FRAMES, D), jnp.float32)
    return base.astype(jnp.bfloat16)


def set_ends(entries, rng, low, high):
    dims = entries.shape
    spot = [jax.random.randint(jax.random.fold_in(rng, axis), (), 0, dims[axis]) for axis in range(len(dims))]
    entries = entries.at[tuple(spot)].set(low)
    longest = dims.index(max(dims))
    spot[longest] = (spot[longest] + 1) % dims[longest]
    return entries.at[tuple(spot)].set(high)


def level_of(own_key, extent, split, smallest, high):
    def one(axis_at, blocks):
        steps = jax.random.uniform(jax.random.fold_in(jax.random.fold_in(own_key, 6), axis_at), (blocks,), jnp.float32, smallest / len(split), high / len(split))
        return jnp.repeat(jnp.exp(steps), extent[axis_at] // blocks).reshape((-1,) + (1,) * (len(extent) - axis_at - 1))

    gain = one(*split[0])
    for cut in split[1:]:
        gain = gain * one(*cut)
    return gain


def split_up(amount, total, limit, skew):
    portions = [(1 << 20) // math.isqrt(rank ** skew) + 1 for rank in range(2, amount + 1)]
    surplus, counts = total - limit - (amount - 1), [1] * (amount - 1)
    while surplus > 0:
        movable = [i for i in range(amount - 1) if counts[i] < limit]
        whole, remaining = sum([portions[i] for i in movable]), surplus
        for i in movable:
            addition = min(limit - counts[i], max(1, remaining * portions[i] // whole), surplus)
            counts[i] = counts[i] + addition
            surplus = surplus - addition
    return np.array([limit] + counts)


def uneven_parts(key, amount, total, reach, skew):
    if amount == 2:
        one = jax.random.randint(key, (), max(1, total - reach), min(reach, total - 1) + 1)
        return jnp.stack([one, total - one])
    sizes = jnp.asarray(split_up(amount, total, reach, skew), jnp.int32)
    pairs = (amount - 1) // 2
    source_of, taker = sizes[1:1 + 2 * pairs:2], sizes[2:2 + 2 * pairs:2]
    room = jnp.minimum(source_of - 1, reach - taker)
    shifted = jax.random.randint(jax.random.fold_in(key, 1), (pairs,), 0, 1 << 20) % (room + 1)
    sizes = sizes.at[1:1 + 2 * pairs:2].set(source_of - shifted).at[2:2 + 2 * pairs:2].set(taker + shifted)
    return sizes[jax.random.permutation(jax.random.fold_in(key, 2), amount)]


def scatter_about(own_key, shape, scale, limit, split=(), held_as=jnp.bfloat16):
    array = scale * jax.random.normal(own_key, shape, jnp.float32)
    if split:
        array = array * level_of(own_key, shape, split, -0.22, 0.18)
    return jnp.clip(array, -limit, limit).astype(held_as)


def setup_inputs(seed: int = 0) -> dict:
    seeds = jax.random.split(jax.random.key(seed), 11)
    return {
        "clean_frames": draw_clean_frames(jax.random.fold_in(seeds[10], 71), 0),
        "noise_frames": scatter_about(seeds[1], (BATCH, FRAMES, D), 1.0, 6.0, ((0, 16), (1, 16))),
        "lengths": set_ends(jax.random.randint(seeds[2], (BATCH,), FRAMES // 4, FRAMES + 1), jax.random.fold_in(seeds[2], 1), FRAMES // 4, FRAMES).astype(jnp.int32),
        "group_ids": jax.vmap(lambda own: jnp.searchsorted(jnp.cumsum(uneven_parts(own, NCHUNK, FRAMES, GROUP, 1)), jnp.arange(FRAMES), side="right"))(jax.random.split(seeds[3], BATCH)).reshape((BATCH, FRAMES)).astype(jnp.int32),
        "time_index": set_ends(jax.random.randint(seeds[4], (BATCH,), 0, TSTEPS), jax.random.fold_in(seeds[4], 1), 0, TSTEPS - 1).astype(jnp.int32),
        "modulation": scatter_about(seeds[5], (D,), 1.0, 4.0, (), jnp.float32),
        "teacher_qkv": scatter_about(seeds[6], (D, 3 * D), D ** -0.5, 0.1875),
        "teacher_out": scatter_about(seeds[7], (D, D), (32.0 / D ** 0.5), 6.0),
        "student_in": scatter_about(seeds[8], (3, D, D), D ** -0.5, 0.1875, ((1, 256),)),
        "student_out": scatter_about(seeds[9], (D, D), (5.0 / D ** 0.5), 1.0, ((0, 256),)),
    }


EPSILON = 1e-06
NEGATIVE = -1e+30
HIGHEST_PREC = lax.Precision.HIGHEST

def normalize(clean_frames, noise_frames, time_index, modulation):
    flow_time = (time_index.astype(jnp.float32) + 0.5) / TSTEPS
    flow_time = flow_time[:, None, None]
    blended = (1.0 - flow_time) * noise_frames.astype(jnp.float32) + flow_time * clean_frames.astype(jnp.float32)
    inv_rms = lax.rsqrt(lax.optimization_barrier(jnp.mean(blended * blended, axis=-1, keepdims=True)) + EPSILON)
    return (blended * inv_rms * (1.0 + flow_time * modulation)).astype(jnp.bfloat16)

def attend_block(queries, key_rows, values, key_bias):
    scores = jnp.dot(queries, key_rows.T, preferred_element_type=jnp.float32) * queries.shape[-1] ** (-0.5)
    scores = scores + key_bias[None, :]
    row_max = lax.optimization_barrier(jnp.max(scores, axis=-1, keepdims=True))
    exponent = jnp.exp(scores - row_max)
    probs_low = (exponent / lax.optimization_barrier(jnp.sum(exponent, axis=-1, keepdims=True))).astype(jnp.bfloat16)
    return jnp.dot(probs_low, values, preferred_element_type=jnp.float32).astype(jnp.bfloat16)

def full_attention(queries, key_rows, values, key_bias):
    total_rows = queries.shape[0]
    block_rows = min(512, total_rows)
    blocked = queries.reshape(total_rows // block_rows, block_rows, queries.shape[1])
    result = lax.map(lambda piece: attend_block(piece, key_rows, values, key_bias), blocked)
    return result.reshape(total_rows, values.shape[1])

def teacher_heads(proj_one, bias_one):
    stacked = jnp.transpose(proj_one, (2, 1, 0, 3))
    result = lax.map(lambda element: full_attention(element[0], element[1], element[2], bias_one), stacked)
    return jnp.transpose(result, (1, 0, 2))

def build_allowed(query_group, query_pos, key_group, key_pos, lengths):
    same_group = key_group[:, None, :] == query_group[:, :, None]
    prev_group = key_group[:, None, :] == query_group[:, :, None] - 1
    live_key = (key_pos[None, :] < lengths[:, None]) & (key_pos[None, :] >= 0)
    itself = key_pos[None, :] == query_pos[:, None]
    return (same_group | prev_group) & (live_key[:, None, :] | itself[None])

def student_probs(queries, key_rows, allowed):
    scores = jnp.einsum('brhd,bwhd->bhrw', queries.astype(jnp.float32), key_rows.astype(jnp.float32), precision=HIGHEST_PREC)
    scores = jnp.where(allowed[:, None], scores * queries.shape[-1] ** (-0.5), NEGATIVE)
    row_max = lax.optimization_barrier(jnp.max(scores, axis=-1, keepdims=True))
    exponent = jnp.exp(scores - row_max)
    return exponent / lax.optimization_barrier(jnp.sum(exponent, axis=-1, keepdims=True))

def rounded(values):
    return lax.optimization_barrier(values.astype(jnp.bfloat16)).astype(jnp.float32)

def fold_window(parts):
    owned_rows = parts[:, :, HALO:HALO + FR_DEV]
    left_rim = parts[:, :, :HALO]
    right_rim = parts[:, :, HALO + FR_DEV:]
    blanks = jnp.zeros_like(left_rim[:1])
    from_prev = jnp.concatenate([blanks, right_rim[:-1]], axis=0)
    from_next = jnp.concatenate([left_rim[1:], blanks], axis=0)
    owned_rows = owned_rows.at[:, :, :HALO].add(from_prev)
    owned_rows = owned_rows.at[:, :, FR_DEV - HALO:].add(from_next)
    return owned_rows

def to_rows(parts):
    return jnp.transpose(parts, (1, 0, 2, 3, 4)).reshape(BATCH * FRAMES, D)

def reference(clean_frames, noise_frames, lengths, group_ids, time_index, modulation, teacher_qkv, teacher_out, student_in, student_out):
    head_dim = D // HEADS
    normed = normalize(clean_frames, noise_frames, time_index, modulation)
    flat_rows = normed.reshape(BATCH * FRAMES, D)
    frame_pos = jnp.arange(FRAMES, dtype=jnp.int32)
    valid = frame_pos[None, :] < lengths[:, None]
    key_bias = jnp.where(valid, 0.0, NEGATIVE).astype(jnp.float32)
    teacher_proj = jnp.dot(flat_rows, teacher_qkv, preferred_element_type=jnp.float32).astype(jnp.bfloat16)
    teacher_proj = teacher_proj.reshape(BATCH, FRAMES, 3, HEADS, head_dim)
    head_out = lax.map(lambda element: teacher_heads(element[0], element[1]), (teacher_proj, key_bias))
    teacher_vel = jnp.dot(head_out.reshape(BATCH * FRAMES, D), teacher_out, preferred_element_type=jnp.float32)

    def project(matrix):
        result = jnp.dot(flat_rows, matrix, preferred_element_type=jnp.float32).astype(jnp.bfloat16)
        return result.reshape(BATCH, FRAMES, HEADS, head_dim)
    query_all = project(student_in[0])
    key_all = project(student_in[1])
    value_all = project(student_in[2])
    padding = ((0, 0), (HALO, HALO), (0, 0), (0, 0))
    key_pad = jnp.pad(key_all, padding)
    value_pad = jnp.pad(value_all, padding)
    group_pad = jnp.pad(group_ids, ((0, 0), (HALO, HALO)), constant_values=-10)
    window = FR_DEV + 2 * HALO

    def block_inputs(block_id):
        offset = block_id * FR_DEV
        queries = lax.dynamic_slice_in_dim(query_all, offset, FR_DEV, 1)
        key_rows = lax.dynamic_slice_in_dim(key_pad, offset, window, 1)
        value_rows = lax.dynamic_slice_in_dim(value_pad, offset, window, 1)
        query_group = lax.dynamic_slice_in_dim(group_ids, offset, FR_DEV, 1)
        key_group = lax.dynamic_slice_in_dim(group_pad, offset, window, 1)
        query_pos = offset + jnp.arange(FR_DEV, dtype=jnp.int32)
        key_pos = offset - HALO + jnp.arange(window, dtype=jnp.int32)
        allowed = build_allowed(query_group, query_pos, key_group, key_pos, lengths)
        return (queries, key_rows, value_rows, allowed)
    block_ids = jnp.arange(N_SEQ, dtype=jnp.int32)

    def forward_block(block_id):
        queries, key_rows, value_rows, allowed = block_inputs(block_id)
        probs = student_probs(queries, key_rows, allowed)
        result = jnp.einsum('bhrw,bwhd->brhd', rounded(probs), value_rows.astype(jnp.float32), precision=HIGHEST_PREC)
        return result.astype(jnp.bfloat16)
    student_mix = to_rows(lax.map(forward_block, block_ids))
    student_vel = jnp.dot(student_mix, student_out, preferred_element_type=jnp.float32)
    difference = jnp.where(valid.reshape(-1)[:, None], student_vel - teacher_vel, 0.0)
    count = jnp.sum(lengths).astype(jnp.float32)
    mean_error = jnp.sum(difference * difference) / (count * D)
    grad_vel = (difference * lax.rsqrt(count)).astype(jnp.bfloat16)
    grad_mix = jnp.dot(grad_vel, student_out.T, preferred_element_type=jnp.float32).astype(jnp.bfloat16)
    grad_mix = grad_mix.reshape(BATCH, FRAMES, HEADS, head_dim)

    def backward_block(block_id):
        queries, key_rows, value_rows, allowed = block_inputs(block_id)
        probs = student_probs(queries, key_rows, allowed)
        upstream = lax.dynamic_slice_in_dim(grad_mix, block_id * FR_DEV, FR_DEV, 1).astype(jnp.float32)
        grad_prob = jnp.einsum('brhd,bwhd->bhrw', upstream, value_rows.astype(jnp.float32), precision=HIGHEST_PREC)
        grad_score = probs * (grad_prob - lax.optimization_barrier(jnp.sum(probs * grad_prob, axis=-1, keepdims=True))) * head_dim ** (-0.5)
        grad_key = jnp.einsum('bhrw,brhd->bwhd', grad_score, queries.astype(jnp.float32), precision=HIGHEST_PREC)
        grad_value = jnp.einsum('bhrw,brhd->bwhd', rounded(probs), upstream, precision=HIGHEST_PREC)
        return (grad_key, grad_value)
    grad_key, grad_value = lax.map(backward_block, block_ids)
    inputs_f32 = flat_rows.astype(jnp.float32)
    grad_k_weight = jnp.dot(inputs_f32.T, to_rows(fold_window(grad_key)), precision=HIGHEST_PREC)
    grad_v_weight = jnp.dot(inputs_f32.T, to_rows(fold_window(grad_value)), precision=HIGHEST_PREC)
    grad_inputs = jnp.stack([grad_k_weight, grad_v_weight])
    return (grad_inputs, mean_error)
```

```python
import jax
import jax.numpy as jnp
from jax import lax
from jax.sharding import PartitionSpec as P

HEADS = 16
HALO = 64
TSTEPS = 1000


EPSILON = 1e-06
NEGATIVE = -1e30


def with_halo(block, sides, width):
    for axis, dim in sides:
        count = lax.axis_size(axis)
        forward = [(i, i + 1) for i in range(count - 1)]
        backward = [(target, source) for source, target in forward]
        low = lax.ppermute(
            lax.slice_in_dim(block, block.shape[dim] - width, None, axis=dim), axis, forward
        )
        high = lax.ppermute(lax.slice_in_dim(block, 0, width, axis=dim), axis, backward)
        block = jnp.concatenate([low, block, high], axis=dim)
    return block


def from_behind(block, axis, distance):
    devices = range(lax.axis_size(axis))
    route = [(i - distance, i) for i in devices if i - distance in devices]
    return lax.ppermute(block, axis, route)


def normalize(clean_frames, noise_frames, time_index, modulation):
    flow_time = (time_index.astype(jnp.float32) + 0.5) / TSTEPS
    flow_time = flow_time[:, None, None]
    blended = (1.0 - flow_time) * noise_frames.astype(
        jnp.float32
    ) + flow_time * clean_frames.astype(jnp.float32)
    inv_rms = lax.rsqrt(jnp.mean(blended * blended, axis=-1, keepdims=True) + EPSILON)
    return (blended * inv_rms * (1.0 + flow_time * modulation)).astype(jnp.bfloat16)


def attend_block(queries, key_rows, values, key_bias):
    scores = jnp.dot(queries, key_rows.T, preferred_element_type=jnp.float32) * queries.shape[
        -1
    ] ** (-0.5)
    scores = scores + key_bias[None, :]
    row_max = jnp.max(scores, axis=-1, keepdims=True)
    exponent = jnp.exp(scores - row_max)
    probs_low = (exponent / jnp.sum(exponent, axis=-1, keepdims=True)).astype(jnp.bfloat16)
    return jnp.dot(probs_low, values, preferred_element_type=jnp.float32).astype(jnp.bfloat16)


def full_attention(queries, key_rows, values, key_bias):
    total_rows = queries.shape[0]
    block_rows = min(512, total_rows)
    blocked = queries.reshape(total_rows // block_rows, block_rows, queries.shape[1])
    result = lax.map(lambda piece: attend_block(piece, key_rows, values, key_bias), blocked)
    return result.reshape(total_rows, values.shape[1])


def teacher_heads(proj_one, bias_one):
    stacked = jnp.transpose(proj_one, (2, 1, 0, 3))
    result = lax.map(
        lambda element: full_attention(element[0], element[1], element[2], bias_one), stacked
    )
    return jnp.transpose(result, (1, 0, 2))


def build_allowed(query_group, query_pos, key_group, key_pos, lengths):
    same_group = key_group[:, None, :] == query_group[:, :, None]
    prev_group = key_group[:, None, :] == query_group[:, :, None] - 1
    live_key = (key_pos[None, :] < lengths[:, None]) & (key_pos[None, :] >= 0)
    itself = key_pos[None, :] == query_pos[:, None]
    return (same_group | prev_group) & (live_key[:, None, :] | itself[None])


def split_product(form, gradient, other, first):
    upper_part = gradient.astype(jnp.bfloat16)
    lower_part = (gradient - upper_part.astype(jnp.float32)).astype(jnp.bfloat16)
    if first:
        return jnp.einsum(form, upper_part, other, preferred_element_type=jnp.float32) + jnp.einsum(
            form, lower_part, other, preferred_element_type=jnp.float32
        )
    return jnp.einsum(form, other, upper_part, preferred_element_type=jnp.float32) + jnp.einsum(
        form, other, lower_part, preferred_element_type=jnp.float32
    )


def total_of(value):
    spread = jnp.broadcast_to(value, (lax.axis_size("seq"), 128))
    spread = lax.all_to_all(spread, "seq", 0, 0, tiled=True).sum(0, keepdims=True)
    spread = jnp.broadcast_to(spread, (lax.axis_size("dp"), 128))
    spread = lax.all_to_all(spread, "dp", 0, 0, tiled=True).sum(0)
    return spread[0]


def shards(
    clean_frames,
    noise_frames,
    lengths,
    group_ids,
    time_index,
    modulation,
    teacher_qkv,
    teacher_out,
    student_in,
    student_out,
):
    dialogs, shard_rows, model_width = clean_frames.shape
    head_dim = model_width // HEADS
    seq_count = lax.axis_size("seq")
    seq_index = lax.axis_index("seq")
    frames = shard_rows * seq_count
    window = shard_rows + 2 * HALO
    rows_each = student_out.shape[0]
    stacked = jnp.concatenate(
        (student_in.reshape(3 * rows_each, model_width), student_out), axis=0
    )
    gathered = lax.all_gather(lax.all_gather(stacked, "seq", axis=0), "dp", axis=0)
    gathered = gathered.reshape(-1, 4 * rows_each, model_width)
    w_inputs = (
        gathered[:, : 3 * rows_each]
        .reshape(-1, 3, rows_each, model_width)
        .transpose(1, 0, 2, 3)
        .reshape(3, -1, model_width)
    )
    w_output = gathered[:, 3 * rows_each :].reshape(-1, model_width)
    frame_count = jnp.sum(lax.all_gather(lengths, "dp", axis=0, tiled=True)).astype(jnp.float32)
    normed = normalize(clean_frames, noise_frames, time_index, modulation)
    flat_rows = normed.reshape(dialogs * shard_rows, model_width)
    frame_pos = jnp.arange(frames, dtype=jnp.int32)
    key_bias = jnp.where(frame_pos[None, :] < lengths[:, None], 0.0, NEGATIVE).astype(jnp.float32)
    teacher_proj = jnp.dot(flat_rows, teacher_qkv, preferred_element_type=jnp.float32).astype(
        jnp.bfloat16
    )
    teacher_proj = teacher_proj.reshape(dialogs, shard_rows, 3, HEADS, head_dim)
    by_heads = lax.all_to_all(teacher_proj, "seq", split_axis=3, concat_axis=1, tiled=True)
    head_out = lax.map(lambda element: teacher_heads(element[0], element[1]), (by_heads, key_bias))
    by_frames = lax.all_to_all(head_out, "seq", split_axis=1, concat_axis=2, tiled=True)
    teacher_vel = jnp.dot(
        by_frames.reshape(dialogs * shard_rows, model_width),
        teacher_out,
        preferred_element_type=jnp.float32,
    )
    offset = seq_index * shard_rows
    queries = jnp.dot(flat_rows, w_inputs[0], preferred_element_type=jnp.float32).astype(
        jnp.bfloat16
    )
    queries = queries.reshape(dialogs, shard_rows, HEADS, head_dim)
    key_local = jnp.dot(flat_rows, w_inputs[1], preferred_element_type=jnp.float32).astype(
        jnp.bfloat16
    )
    value_local = jnp.dot(flat_rows, w_inputs[2], preferred_element_type=jnp.float32).astype(
        jnp.bfloat16
    )
    both_local = jnp.concatenate((key_local, value_local), axis=-1).reshape(
        dialogs, shard_rows, 2 * model_width
    )
    both_window = with_halo(both_local, (("seq", 1),), HALO)
    key_rows = both_window[:, :, :model_width].reshape(dialogs, window, HEADS, head_dim)
    value_rows = both_window[:, :, model_width:].reshape(dialogs, window, HEADS, head_dim)
    group_pad = jnp.pad(group_ids, ((0, 0), (HALO, HALO)), constant_values=-10)
    key_group = lax.dynamic_slice_in_dim(group_pad, offset, window, 1)
    query_group = lax.dynamic_slice_in_dim(group_ids, offset, shard_rows, 1)
    query_pos = offset + jnp.arange(shard_rows, dtype=jnp.int32)
    key_pos = offset - HALO + jnp.arange(window, dtype=jnp.int32)
    allowed = build_allowed(query_group, query_pos, key_group, key_pos, lengths)
    scaling = head_dim ** (-0.5)
    scores = jnp.einsum("brhd,bwhd->bhrw", queries, key_rows, preferred_element_type=jnp.float32)
    scores = jnp.where(allowed[:, None], scores * scaling, NEGATIVE)
    row_max = jnp.max(scores, axis=-1, keepdims=True)
    exponent = jnp.exp(scores - row_max)
    probs = exponent / jnp.sum(exponent, axis=-1, keepdims=True)
    probs_low = probs.astype(jnp.bfloat16)
    student_mix = jnp.einsum(
        "bhrw,bwhd->brhd", probs_low, value_rows, preferred_element_type=jnp.float32
    ).astype(jnp.bfloat16)
    mix_flat = student_mix.reshape(dialogs * shard_rows, model_width)
    student_vel = jnp.dot(mix_flat, w_output, preferred_element_type=jnp.float32)
    query_valid = (query_pos[None, :] < lengths[:, None]).reshape(-1)
    difference = jnp.where(query_valid[:, None], student_vel - teacher_vel, 0.0)
    square_sum = total_of(jnp.sum(difference * difference))
    mean_error = square_sum / (frame_count * model_width)
    grad_vel = (difference * lax.rsqrt(frame_count)).astype(jnp.bfloat16)
    grad_mix = jnp.dot(grad_vel, w_output.T, preferred_element_type=jnp.float32).astype(
        jnp.bfloat16
    )
    grad_mix = grad_mix.reshape(dialogs, shard_rows, HEADS, head_dim)
    grad_prob = jnp.einsum(
        "brhd,bwhd->bhrw", grad_mix, value_rows, preferred_element_type=jnp.float32
    )
    grad_score = probs * (grad_prob - jnp.sum(probs * grad_prob, axis=-1, keepdims=True)) * scaling
    grad_key = split_product("bhrw,brhd->bwhd", grad_score, queries, True)
    grad_value = jnp.einsum(
        "bhrw,brhd->bwhd", probs_low, grad_mix, preferred_element_type=jnp.float32
    )
    grad_both = jnp.concatenate(
        (
            grad_key.reshape(dialogs, window, model_width),
            grad_value.reshape(dialogs, window, model_width),
        ),
        axis=-1,
    )
    from_next = from_behind(grad_both[:, :HALO].astype(jnp.bfloat16), "seq", -1).astype(jnp.float32)
    from_prev = from_behind(
        grad_both[:, HALO + shard_rows :].astype(jnp.bfloat16), "seq", 1
    ).astype(jnp.float32)
    owned_rows = grad_both[:, HALO : HALO + shard_rows]
    owned_rows = owned_rows.at[:, :HALO].add(from_prev)
    owned_rows = owned_rows.at[:, shard_rows - HALO :].add(from_next)
    by_head = owned_rows.reshape(shard_rows, 2, HEADS, head_dim).transpose(0, 2, 1, 3)
    head_grads = lax.all_to_all(by_head, "seq", split_axis=1, concat_axis=0, tiled=True)
    head_grads = head_grads.reshape(frames, 2 * head_dim)
    normed_all = lax.all_gather(flat_rows, "seq", axis=0, tiled=True)
    partial = split_product("rf,rg->fg", head_grads, normed_all, False)
    dp_count = lax.axis_size("dp")
    partial = partial.reshape(dp_count, seq_count, rows_each, 2 * head_dim)
    partial = lax.all_to_all(partial, "dp", split_axis=0, concat_axis=0, tiled=True).sum(0)
    mine = lax.all_to_all(partial, "seq", split_axis=0, concat_axis=0, tiled=True)
    mine = mine.reshape(HEADS, rows_each, 2, head_dim).transpose(2, 1, 0, 3)
    grad_inputs = mine.reshape(2, rows_each, model_width)
    return (grad_inputs, mean_error)


def solution(mesh):
    in_specs = (
        P("dp", "seq", None),
        P("dp", "seq", None),
        P("dp"),
        P("dp", None),
        P("dp"),
        P(),
        P(),
        P(),
        P(None, ("dp", "seq"), None),
        P(("dp", "seq"), None),
    )
    out_specs = (P(None, ("dp", "seq"), None), P())
    return jax.shard_map(shards, mesh=mesh, in_specs=in_specs, out_specs=out_specs, check_vma=False)
```

```python
import jax
import jax.numpy as jnp
from jax import lax
from jax.sharding import PartitionSpec as P

HEADS = 16
HALO = 64
TSTEPS = 1000


EPSILON = 1e-06
NEGATIVE = -1e30


def with_halo(block, sides, width):
    for axis, dim in sides:
        count = lax.axis_size(axis)
        forward = [(i, i + 1) for i in range(count - 1)]
        backward = [(target, source) for source, target in forward]
        low = lax.ppermute(
            lax.slice_in_dim(block, block.shape[dim] - width, None, axis=dim), axis, forward
        )
        high = lax.ppermute(lax.slice_in_dim(block, 0, width, axis=dim), axis, backward)
        block = jnp.concatenate([low, block, high], axis=dim)
    return block


def from_behind(block, axis, distance):
    devices = range(lax.axis_size(axis))
    route = [(i - distance, i) for i in devices if i - distance in devices]
    return lax.ppermute(block, axis, route)


def normalize(clean_frames, noise_frames, time_index, modulation):
    flow_time = (time_index.astype(jnp.float32) + 0.5) / TSTEPS
    flow_time = flow_time[:, None, None]
    blended = (1.0 - flow_time) * noise_frames.astype(
        jnp.float32
    ) + flow_time * clean_frames.astype(jnp.float32)
    inv_rms = lax.rsqrt(jnp.mean(blended * blended, axis=-1, keepdims=True) + EPSILON)
    return (blended * inv_rms * (1.0 + flow_time * modulation)).astype(jnp.bfloat16)


def attend_block(queries, key_rows, values, key_bias):
    scores = jnp.dot(queries, key_rows.T, preferred_element_type=jnp.float32) * queries.shape[
        -1
    ] ** (-0.5)
    scores = scores + key_bias[None, :]
    row_max = jnp.max(scores, axis=-1, keepdims=True)
    exponent = jnp.exp(scores - row_max)
    probs_low = (exponent / jnp.sum(exponent, axis=-1, keepdims=True)).astype(jnp.bfloat16)
    return jnp.dot(probs_low, values, preferred_element_type=jnp.float32).astype(jnp.bfloat16)


def full_attention(queries, key_rows, values, key_bias):
    total_rows = queries.shape[0]
    block_rows = min(512, total_rows)
    blocked = queries.reshape(total_rows // block_rows, block_rows, queries.shape[1])
    result = lax.map(lambda piece: attend_block(piece, key_rows, values, key_bias), blocked)
    return result.reshape(total_rows, values.shape[1])


def teacher_heads(proj_one, bias_one):
    stacked = jnp.transpose(proj_one, (2, 1, 0, 3))
    result = lax.map(
        lambda element: full_attention(element[0], element[1], element[2], bias_one), stacked
    )
    return jnp.transpose(result, (1, 0, 2))


def build_allowed(query_group, query_pos, key_group, key_pos, lengths):
    same_group = key_group[:, None, :] == query_group[:, :, None]
    prev_group = key_group[:, None, :] == query_group[:, :, None] - 1
    live_key = (key_pos[None, :] < lengths[:, None]) & (key_pos[None, :] >= 0)
    itself = key_pos[None, :] == query_pos[:, None]
    return (same_group | prev_group) & (live_key[:, None, :] | itself[None])


def split_product(form, gradient, other, first):
    upper_part = gradient.astype(jnp.bfloat16)
    lower_part = (gradient - upper_part.astype(jnp.float32)).astype(jnp.bfloat16)
    if first:
        return jnp.einsum(form, upper_part, other, preferred_element_type=jnp.float32) + jnp.einsum(
            form, lower_part, other, preferred_element_type=jnp.float32
        )
    return jnp.einsum(form, other, upper_part, preferred_element_type=jnp.float32) + jnp.einsum(
        form, other, lower_part, preferred_element_type=jnp.float32
    )


def shards(
    clean_frames,
    noise_frames,
    lengths,
    group_ids,
    time_index,
    modulation,
    teacher_qkv,
    teacher_out,
    student_in,
    student_out,
):
    dialogs, shard_rows, model_width = clean_frames.shape
    head_dim = model_width // HEADS
    seq_count = lax.axis_size("seq")
    seq_index = lax.axis_index("seq")
    frames = shard_rows * seq_count
    window = shard_rows + 2 * HALO
    rows_each = student_out.shape[0]
    stacked = jnp.concatenate((student_in, student_out[None]), axis=0)
    gathered = lax.all_gather(
        lax.all_gather(stacked, "seq", axis=1, tiled=True), "dp", axis=1, tiled=True
    )
    w_inputs = gathered[:3]
    w_output = gathered[3]
    normed = normalize(clean_frames, noise_frames, time_index, modulation)
    flat_rows = normed.reshape(dialogs * shard_rows, model_width)
    frame_pos = jnp.arange(frames, dtype=jnp.int32)
    key_bias = jnp.where(frame_pos[None, :] < lengths[:, None], 0.0, NEGATIVE).astype(jnp.float32)
    teacher_proj = jnp.dot(flat_rows, teacher_qkv, preferred_element_type=jnp.float32).astype(
        jnp.bfloat16
    )
    teacher_proj = teacher_proj.reshape(dialogs, shard_rows, 3, HEADS, head_dim)
    by_heads = lax.all_to_all(teacher_proj, "seq", split_axis=3, concat_axis=1, tiled=True)
    head_out = lax.map(lambda element: teacher_heads(element[0], element[1]), (by_heads, key_bias))
    by_frames = lax.all_to_all(head_out, "seq", split_axis=1, concat_axis=2, tiled=True)
    teacher_vel = jnp.dot(
        by_frames.reshape(dialogs * shard_rows, model_width),
        teacher_out,
        preferred_element_type=jnp.float32,
    )
    offset = seq_index * shard_rows
    queries = jnp.dot(flat_rows, w_inputs[0], preferred_element_type=jnp.float32).astype(
        jnp.bfloat16
    )
    queries = queries.reshape(dialogs, shard_rows, HEADS, head_dim)
    key_local = jnp.dot(flat_rows, w_inputs[1], preferred_element_type=jnp.float32).astype(
        jnp.bfloat16
    )
    value_local = jnp.dot(flat_rows, w_inputs[2], preferred_element_type=jnp.float32).astype(
        jnp.bfloat16
    )
    both_local = jnp.concatenate((key_local, value_local), axis=-1).reshape(
        dialogs, shard_rows, 2 * model_width
    )
    both_window = with_halo(both_local, (("seq", 1),), HALO)
    key_rows = both_window[:, :, :model_width].reshape(dialogs, window, HEADS, head_dim)
    value_rows = both_window[:, :, model_width:].reshape(dialogs, window, HEADS, head_dim)
    group_pad = jnp.pad(group_ids, ((0, 0), (HALO, HALO)), constant_values=-10)
    key_group = lax.dynamic_slice_in_dim(group_pad, offset, window, 1)
    query_group = lax.dynamic_slice_in_dim(group_ids, offset, shard_rows, 1)
    query_pos = offset + jnp.arange(shard_rows, dtype=jnp.int32)
    key_pos = offset - HALO + jnp.arange(window, dtype=jnp.int32)
    allowed = build_allowed(query_group, query_pos, key_group, key_pos, lengths)
    scaling = head_dim ** (-0.5)
    scores = jnp.einsum("brhd,bwhd->bhrw", queries, key_rows, preferred_element_type=jnp.float32)
    scores = jnp.where(allowed[:, None], scores * scaling, NEGATIVE)
    row_max = jnp.max(scores, axis=-1, keepdims=True)
    exponent = jnp.exp(scores - row_max)
    probs = exponent / jnp.sum(exponent, axis=-1, keepdims=True)
    probs_low = probs.astype(jnp.bfloat16)
    student_mix = jnp.einsum(
        "bhrw,bwhd->brhd", probs_low, value_rows, preferred_element_type=jnp.float32
    ).astype(jnp.bfloat16)
    mix_flat = student_mix.reshape(dialogs * shard_rows, model_width)
    student_vel = jnp.dot(mix_flat, w_output, preferred_element_type=jnp.float32)
    query_valid = (query_pos[None, :] < lengths[:, None]).reshape(-1)
    difference = jnp.where(query_valid[:, None], student_vel - teacher_vel, 0.0)
    square_local = jnp.sum(difference * difference)
    count_local = jnp.sum(query_valid.astype(jnp.float32))
    grad_vel = difference.astype(jnp.bfloat16)
    grad_mix = jnp.dot(grad_vel, w_output.T, preferred_element_type=jnp.float32).astype(
        jnp.bfloat16
    )
    grad_mix = grad_mix.reshape(dialogs, shard_rows, HEADS, head_dim)
    grad_prob = jnp.einsum(
        "brhd,bwhd->bhrw", grad_mix, value_rows, preferred_element_type=jnp.float32
    )
    grad_score = probs * (grad_prob - jnp.sum(probs * grad_prob, axis=-1, keepdims=True)) * scaling
    grad_key = split_product("bhrw,brhd->bwhd", grad_score, queries, True)
    grad_value = jnp.einsum(
        "bhrw,brhd->bwhd", probs_low, grad_mix, preferred_element_type=jnp.float32
    )
    grad_both = jnp.concatenate(
        (
            grad_key.reshape(dialogs, window, model_width),
            grad_value.reshape(dialogs, window, model_width),
        ),
        axis=-1,
    )
    from_next = from_behind(grad_both[:, :HALO].astype(jnp.bfloat16), "seq", -1).astype(jnp.float32)
    from_prev = from_behind(
        grad_both[:, HALO + shard_rows :].astype(jnp.bfloat16), "seq", 1
    ).astype(jnp.float32)
    owned_rows = grad_both[:, HALO : HALO + shard_rows]
    owned_rows = owned_rows.at[:, :HALO].add(from_prev)
    owned_rows = owned_rows.at[:, shard_rows - HALO :].add(from_next)
    by_head = owned_rows.reshape(shard_rows, 2, HEADS, head_dim).transpose(0, 2, 1, 3)
    head_grads = lax.all_to_all(by_head, "seq", split_axis=1, concat_axis=0, tiled=True)
    head_grads = head_grads.reshape(frames, 2 * head_dim)
    normed_all = lax.all_gather(flat_rows, "seq", axis=0, tiled=True)
    partial = split_product("rf,rg->fg", head_grads, normed_all, False)
    dp_count = lax.axis_size("dp")
    partial = partial.reshape(dp_count, seq_count, rows_each, 2 * head_dim)
    lane = jnp.arange(2 * head_dim)
    scalars = jnp.where(lane == 0, square_local, jnp.where(lane == 1, count_local, 0.0))
    scalars = jnp.broadcast_to(scalars, (dp_count, seq_count, 1, 2 * head_dim))
    partial = jnp.concatenate((partial, scalars), axis=2)
    partial = lax.all_to_all(partial, "dp", split_axis=0, concat_axis=0, tiled=True).sum(0)
    mine = lax.all_to_all(partial, "seq", split_axis=0, concat_axis=0, tiled=True)
    totals = mine[:, rows_each].sum(0)
    square_sum, frame_count = totals[0], totals[1]
    mean_error = square_sum / (frame_count * model_width)
    mine = mine[:, :rows_each] * lax.rsqrt(frame_count)
    mine = mine.reshape(HEADS, rows_each, 2, head_dim).transpose(2, 1, 0, 3)
    grad_inputs = mine.reshape(2, rows_each, model_width)
    return (grad_inputs, mean_error)


def solution(mesh):
    in_specs = (
        P("dp", "seq", None),
        P("dp", "seq", None),
        P("dp"),
        P("dp", None),
        P("dp"),
        P(),
        P(),
        P(),
        P(None, ("dp", "seq"), None),
        P(("dp", "seq"), None),
    )
    out_specs = (P(None, ("dp", "seq"), None), P())
    return jax.shard_map(shards, mesh=mesh, in_specs=in_specs, out_specs=out_specs, check_vma=False)
```

```python
import jax
import jax.numpy as jnp
from jax import lax
from jax.sharding import PartitionSpec as P

HEADS = 16
HALO = 64
TSTEPS = 1000


EPSILON = 1e-06
NEGATIVE = -1e30


def with_halo(block, sides, width):
    for axis, dim in sides:
        count = lax.axis_size(axis)
        forward = [(i, i + 1) for i in range(count - 1)]
        backward = [(target, source) for source, target in forward]
        low = lax.ppermute(
            lax.slice_in_dim(block, block.shape[dim] - width, None, axis=dim), axis, forward
        )
        high = lax.ppermute(lax.slice_in_dim(block, 0, width, axis=dim), axis, backward)
        block = jnp.concatenate([low, block, high], axis=dim)
    return block


def from_behind(block, axis, distance):
    devices = range(lax.axis_size(axis))
    route = [(i - distance, i) for i in devices if i - distance in devices]
    return lax.ppermute(block, axis, route)


def normalize(clean_frames, noise_frames, time_index, modulation):
    flow_time = (time_index.astype(jnp.float32) + 0.5) / TSTEPS
    flow_time = flow_time[:, None, None]
    blended = (1.0 - flow_time) * noise_frames.astype(
        jnp.float32
    ) + flow_time * clean_frames.astype(jnp.float32)
    inv_rms = lax.rsqrt(jnp.mean(blended * blended, axis=-1, keepdims=True) + EPSILON)
    return (blended * inv_rms * (1.0 + flow_time * modulation)).astype(jnp.bfloat16)


def attend_block(queries, key_rows, values, key_bias):
    scores = jnp.dot(queries, key_rows.T, preferred_element_type=jnp.float32) * queries.shape[
        -1
    ] ** (-0.5)
    scores = scores + key_bias[None, :]
    row_max = jnp.max(scores, axis=-1, keepdims=True)
    exponent = jnp.exp(scores - row_max)
    probs_low = (exponent / jnp.sum(exponent, axis=-1, keepdims=True)).astype(jnp.bfloat16)
    return jnp.dot(probs_low, values, preferred_element_type=jnp.float32).astype(jnp.bfloat16)


def full_attention(queries, key_rows, values, key_bias):
    total_rows = queries.shape[0]
    block_rows = min(512, total_rows)
    blocked = queries.reshape(total_rows // block_rows, block_rows, queries.shape[1])
    result = lax.map(lambda piece: attend_block(piece, key_rows, values, key_bias), blocked)
    return result.reshape(total_rows, values.shape[1])


def teacher_heads(proj_one, bias_one):
    stacked = jnp.transpose(proj_one, (2, 1, 0, 3))
    result = lax.map(
        lambda element: full_attention(element[0], element[1], element[2], bias_one), stacked
    )
    return jnp.transpose(result, (1, 0, 2))


def teacher_direct(proj_one, bias_one):
    def one_head(part):
        return attend_block(part[:, 0], part[:, 1], part[:, 2], bias_one)

    return jax.vmap(one_head, in_axes=2, out_axes=1)(proj_one)


def build_allowed(query_group, query_pos, key_group, key_pos, lengths):
    same_group = key_group[:, None, :] == query_group[:, :, None]
    prev_group = key_group[:, None, :] == query_group[:, :, None] - 1
    live_key = (key_pos[None, :] < lengths[:, None]) & (key_pos[None, :] >= 0)
    itself = key_pos[None, :] == query_pos[:, None]
    return (same_group | prev_group) & (live_key[:, None, :] | itself[None])


def split_product(form, gradient, other, first):
    upper_part = gradient.astype(jnp.bfloat16)
    lower_part = (gradient - upper_part.astype(jnp.float32)).astype(jnp.bfloat16)
    if first:
        return jnp.einsum(form, upper_part, other, preferred_element_type=jnp.float32) + jnp.einsum(
            form, lower_part, other, preferred_element_type=jnp.float32
        )
    return jnp.einsum(form, other, upper_part, preferred_element_type=jnp.float32) + jnp.einsum(
        form, other, lower_part, preferred_element_type=jnp.float32
    )


def shards(
    clean_frames,
    noise_frames,
    lengths,
    group_ids,
    time_index,
    modulation,
    teacher_qkv,
    teacher_out,
    student_in,
    student_out,
):
    dialogs, shard_rows, model_width = clean_frames.shape
    head_dim = model_width // HEADS
    seq_count = lax.axis_size("seq")
    seq_index = lax.axis_index("seq")
    frames = shard_rows * seq_count
    window = shard_rows + 2 * HALO
    rows_each = student_out.shape[0]
    stacked = jnp.concatenate((student_in, student_out[None]), axis=0)
    gathered = lax.all_gather(
        lax.all_gather(stacked, "seq", axis=1, tiled=True), "dp", axis=1, tiled=True
    )
    w_inputs = gathered[:3]
    w_output = gathered[3]
    normed = normalize(clean_frames, noise_frames, time_index, modulation)
    flat_rows = normed.reshape(dialogs * shard_rows, model_width)
    frame_pos = jnp.arange(frames, dtype=jnp.int32)
    key_bias = jnp.where(frame_pos[None, :] < lengths[:, None], 0.0, NEGATIVE).astype(jnp.float32)
    teacher_proj = jnp.dot(flat_rows, teacher_qkv, preferred_element_type=jnp.float32).astype(
        jnp.bfloat16
    )
    teacher_proj = teacher_proj.reshape(dialogs, shard_rows, 3, HEADS, head_dim)
    by_heads = lax.all_to_all(teacher_proj, "seq", split_axis=3, concat_axis=1, tiled=True)
    head_out = jax.vmap(teacher_direct)(by_heads, key_bias)
    by_frames = lax.all_to_all(head_out, "seq", split_axis=1, concat_axis=2, tiled=True)
    teacher_vel = jnp.dot(
        by_frames.reshape(dialogs * shard_rows, model_width),
        teacher_out,
        preferred_element_type=jnp.float32,
    )
    offset = seq_index * shard_rows
    queries = jnp.dot(flat_rows, w_inputs[0], preferred_element_type=jnp.float32).astype(
        jnp.bfloat16
    )
    queries = queries.reshape(dialogs, shard_rows, HEADS, head_dim)
    key_local = jnp.dot(flat_rows, w_inputs[1], preferred_element_type=jnp.float32).astype(
        jnp.bfloat16
    )
    value_local = jnp.dot(flat_rows, w_inputs[2], preferred_element_type=jnp.float32).astype(
        jnp.bfloat16
    )
    both_local = jnp.concatenate((key_local, value_local), axis=-1).reshape(
        dialogs, shard_rows, 2 * model_width
    )
    both_window = with_halo(both_local, (("seq", 1),), HALO)
    key_rows = both_window[:, :, :model_width].reshape(dialogs, window, HEADS, head_dim)
    value_rows = both_window[:, :, model_width:].reshape(dialogs, window, HEADS, head_dim)
    group_pad = jnp.pad(group_ids, ((0, 0), (HALO, HALO)), constant_values=-10)
    key_group = lax.dynamic_slice_in_dim(group_pad, offset, window, 1)
    query_group = lax.dynamic_slice_in_dim(group_ids, offset, shard_rows, 1)
    query_pos = offset + jnp.arange(shard_rows, dtype=jnp.int32)
    key_pos = offset - HALO + jnp.arange(window, dtype=jnp.int32)
    allowed = build_allowed(query_group, query_pos, key_group, key_pos, lengths)
    scaling = head_dim ** (-0.5)
    scores = jnp.einsum("brhd,bwhd->bhrw", queries, key_rows, preferred_element_type=jnp.float32)
    scores = jnp.where(allowed[:, None], scores * scaling, NEGATIVE)
    row_max = jnp.max(scores, axis=-1, keepdims=True)
    exponent = jnp.exp(scores - row_max)
    probs = exponent / jnp.sum(exponent, axis=-1, keepdims=True)
    probs_low = probs.astype(jnp.bfloat16)
    student_mix = jnp.einsum(
        "bhrw,bwhd->brhd", probs_low, value_rows, preferred_element_type=jnp.float32
    ).astype(jnp.bfloat16)
    mix_flat = student_mix.reshape(dialogs * shard_rows, model_width)
    student_vel = jnp.dot(mix_flat, w_output, preferred_element_type=jnp.float32)
    query_valid = (query_pos[None, :] < lengths[:, None]).reshape(-1)
    difference = jnp.where(query_valid[:, None], student_vel - teacher_vel, 0.0)
    square_local = jnp.sum(difference * difference)
    count_local = jnp.sum(query_valid.astype(jnp.float32))
    grad_vel = difference.astype(jnp.bfloat16)
    grad_mix = jnp.dot(grad_vel, w_output.T, preferred_element_type=jnp.float32).astype(
        jnp.bfloat16
    )
    grad_mix = grad_mix.reshape(dialogs, shard_rows, HEADS, head_dim)
    grad_prob = jnp.einsum(
        "brhd,bwhd->bhrw", grad_mix, value_rows, preferred_element_type=jnp.float32
    )
    grad_score = probs * (grad_prob - jnp.sum(probs * grad_prob, axis=-1, keepdims=True)) * scaling
    grad_score = lax.optimization_barrier(grad_score)
    grad_key = split_product("bhrw,brhd->bwhd", grad_score, queries, True)
    grad_value = jnp.einsum(
        "bhrw,brhd->bwhd", probs_low, grad_mix, preferred_element_type=jnp.float32
    )
    grad_both = jnp.concatenate(
        (
            grad_key.reshape(dialogs, window, model_width),
            grad_value.reshape(dialogs, window, model_width),
        ),
        axis=-1,
    )
    from_next = from_behind(grad_both[:, :HALO].astype(jnp.bfloat16), "seq", -1).astype(jnp.float32)
    from_prev = from_behind(
        grad_both[:, HALO + shard_rows :].astype(jnp.bfloat16), "seq", 1
    ).astype(jnp.float32)
    owned_rows = grad_both[:, HALO : HALO + shard_rows]
    owned_rows = owned_rows.at[:, :HALO].add(from_prev)
    owned_rows = owned_rows.at[:, shard_rows - HALO :].add(from_next)
    by_head = owned_rows.reshape(shard_rows, 2, HEADS, head_dim).transpose(0, 2, 1, 3)
    head_grads = lax.all_to_all(by_head, "seq", split_axis=1, concat_axis=0, tiled=True)
    head_grads = head_grads.reshape(frames, 2 * head_dim)
    normed_all = lax.all_gather(flat_rows, "seq", axis=0, tiled=True)
    partial = split_product("rf,rg->fg", head_grads, normed_all, False)
    dp_count = lax.axis_size("dp")
    partial = partial.reshape(dp_count, -1)
    lane = jnp.arange(2 * head_dim)
    scalars = jnp.where(lane == 0, square_local, jnp.where(lane == 1, count_local, 0.0))
    partial = jnp.concatenate(
        (partial, jnp.broadcast_to(scalars, (dp_count, 2 * head_dim))), axis=1
    )
    partial = lax.all_to_all(partial, "dp", split_axis=0, concat_axis=0, tiled=True).sum(0)
    block = rows_each * 2 * head_dim
    partial = jnp.concatenate(
        (
            partial[: seq_count * block].reshape(seq_count, block),
            jnp.broadcast_to(partial[seq_count * block :], (seq_count, 2 * head_dim)),
        ),
        axis=1,
    )
    mine = lax.all_to_all(partial, "seq", split_axis=0, concat_axis=0, tiled=True)
    totals = mine[:, block:].sum(0)
    square_sum, frame_count = totals[0], totals[1]
    mean_error = square_sum / (frame_count * model_width)
    mine = mine[:, :block] * lax.rsqrt(frame_count)
    mine = mine.reshape(HEADS, rows_each, 2, head_dim).transpose(2, 1, 0, 3)
    grad_inputs = mine.reshape(2, rows_each, model_width)
    return (grad_inputs, mean_error)


def solution(mesh):
    in_specs = (
        P("dp", "seq", None),
        P("dp", "seq", None),
        P("dp"),
        P("dp", None),
        P("dp"),
        P(),
        P(),
        P(),
        P(None, ("dp", "seq"), None),
        P(("dp", "seq"), None),
    )
    out_specs = (P(None, ("dp", "seq"), None), P())
    return jax.shard_map(shards, mesh=mesh, in_specs=in_specs, out_specs=out_specs, check_vma=False)
```

```python
import jax
import jax.numpy as jnp
from jax import lax
from jax.sharding import PartitionSpec as P

HEADS = 16
HALO = 64
TSTEPS = 1000


EPSILON = 1e-06
NEGATIVE = -1e30


def with_halo(block, sides, width):
    for axis, dim in sides:
        count = lax.axis_size(axis)
        forward = [(i, i + 1) for i in range(count - 1)]
        backward = [(target, source) for source, target in forward]
        low = lax.ppermute(
            lax.slice_in_dim(block, block.shape[dim] - width, None, axis=dim), axis, forward
        )
        high = lax.ppermute(lax.slice_in_dim(block, 0, width, axis=dim), axis, backward)
        block = jnp.concatenate([low, block, high], axis=dim)
    return block


def from_behind(block, axis, distance):
    devices = range(lax.axis_size(axis))
    route = [(i - distance, i) for i in devices if i - distance in devices]
    return lax.ppermute(block, axis, route)


def normalize(clean_frames, noise_frames, time_index, modulation):
    flow_time = (time_index.astype(jnp.float32) + 0.5) / TSTEPS
    flow_time = flow_time[:, None, None]
    blended = (1.0 - flow_time) * noise_frames.astype(
        jnp.float32
    ) + flow_time * clean_frames.astype(jnp.float32)
    inv_rms = lax.rsqrt(jnp.mean(blended * blended, axis=-1, keepdims=True) + EPSILON)
    return (blended * inv_rms * (1.0 + flow_time * modulation)).astype(jnp.bfloat16)


def attend_block(queries, key_rows, values, key_bias):
    scores = jnp.dot(queries, key_rows.T, preferred_element_type=jnp.float32) * queries.shape[
        -1
    ] ** (-0.5)
    scores = scores + key_bias[None, :]
    row_max = jnp.max(scores, axis=-1, keepdims=True)
    exponent = jnp.exp(scores - row_max)
    probs_low = (exponent / jnp.sum(exponent, axis=-1, keepdims=True)).astype(jnp.bfloat16)
    return jnp.dot(probs_low, values, preferred_element_type=jnp.float32).astype(jnp.bfloat16)


def full_attention(queries, key_rows, values, key_bias):
    total_rows = queries.shape[0]
    block_rows = min(512, total_rows)
    blocked = queries.reshape(total_rows // block_rows, block_rows, queries.shape[1])
    result = lax.map(lambda piece: attend_block(piece, key_rows, values, key_bias), blocked)
    return result.reshape(total_rows, values.shape[1])


def teacher_heads(proj_one, bias_one):
    stacked = jnp.transpose(proj_one, (2, 1, 0, 3))
    result = lax.map(
        lambda element: full_attention(element[0], element[1], element[2], bias_one), stacked
    )
    return jnp.transpose(result, (1, 0, 2))


def teacher_direct(proj_one, bias_one):
    def one_head(part):
        return attend_block(part[:, 0], part[:, 1], part[:, 2], bias_one)

    return jax.vmap(one_head, in_axes=2, out_axes=1)(proj_one)


def build_allowed(query_group, query_pos, key_group, key_pos, lengths):
    same_group = key_group[:, None, :] == query_group[:, :, None]
    prev_group = key_group[:, None, :] == query_group[:, :, None] - 1
    live_key = (key_pos[None, :] < lengths[:, None]) & (key_pos[None, :] >= 0)
    itself = key_pos[None, :] == query_pos[:, None]
    return (same_group | prev_group) & (live_key[:, None, :] | itself[None])


def split_product(form, gradient, other, first):
    upper_part = gradient.astype(jnp.bfloat16)
    lower_part = (gradient - upper_part.astype(jnp.float32)).astype(jnp.bfloat16)
    if first:
        return jnp.einsum(form, upper_part, other, preferred_element_type=jnp.float32) + jnp.einsum(
            form, lower_part, other, preferred_element_type=jnp.float32
        )
    return jnp.einsum(form, other, upper_part, preferred_element_type=jnp.float32) + jnp.einsum(
        form, other, lower_part, preferred_element_type=jnp.float32
    )


def shards(
    clean_frames,
    noise_frames,
    lengths,
    group_ids,
    time_index,
    modulation,
    teacher_qkv,
    teacher_out,
    student_in,
    student_out,
):
    dialogs, shard_rows, model_width = clean_frames.shape
    head_dim = model_width // HEADS
    seq_count = lax.axis_size("seq")
    seq_index = lax.axis_index("seq")
    frames = shard_rows * seq_count
    window = shard_rows + 2 * HALO
    rows_each = student_out.shape[0]
    stacked = jnp.concatenate((student_in, student_out[None]), axis=0)
    gathered = lax.all_gather(
        lax.all_gather(stacked, "seq", axis=1, tiled=True), "dp", axis=1, tiled=True
    )
    w_inputs = gathered[:3]
    w_output = gathered[3]
    normed = normalize(clean_frames, noise_frames, time_index, modulation)
    flat_rows = normed.reshape(dialogs * shard_rows, model_width)
    frame_pos = jnp.arange(frames, dtype=jnp.int32)
    key_bias = jnp.where(frame_pos[None, :] < lengths[:, None], 0.0, NEGATIVE).astype(jnp.float32)
    teacher_proj = jnp.dot(flat_rows, teacher_qkv, preferred_element_type=jnp.float32).astype(
        jnp.bfloat16
    )
    teacher_proj = teacher_proj.reshape(dialogs, shard_rows, 3, HEADS, head_dim)
    by_heads = lax.all_to_all(teacher_proj, "seq", split_axis=3, concat_axis=1, tiled=True)
    head_out = jax.vmap(teacher_direct)(by_heads, key_bias)
    heads_here = head_out.shape[2]
    head_out = head_out.reshape(dialogs, seq_count, shard_rows, heads_here, head_dim)
    by_frames = lax.all_to_all(head_out, "seq", split_axis=1, concat_axis=1, tiled=True)
    teacher_vel = jnp.einsum(
        "bsfhd,shdn->bfn",
        by_frames,
        teacher_out.reshape(seq_count, heads_here, head_dim, model_width),
        preferred_element_type=jnp.float32,
    ).reshape(dialogs * shard_rows, model_width)
    offset = seq_index * shard_rows
    queries = jnp.dot(flat_rows, w_inputs[0], preferred_element_type=jnp.float32).astype(
        jnp.bfloat16
    )
    queries = queries.reshape(dialogs, shard_rows, HEADS, head_dim)
    key_local = jnp.dot(flat_rows, w_inputs[1], preferred_element_type=jnp.float32).astype(
        jnp.bfloat16
    )
    value_local = jnp.dot(flat_rows, w_inputs[2], preferred_element_type=jnp.float32).astype(
        jnp.bfloat16
    )
    both_local = jnp.concatenate((key_local, value_local), axis=-1).reshape(
        dialogs, shard_rows, 2 * model_width
    )
    both_window = with_halo(both_local, (("seq", 1),), HALO)
    key_rows = both_window[:, :, :model_width].reshape(dialogs, window, HEADS, head_dim)
    value_rows = both_window[:, :, model_width:].reshape(dialogs, window, HEADS, head_dim)
    group_pad = jnp.pad(group_ids, ((0, 0), (HALO, HALO)), constant_values=-10)
    key_group = lax.dynamic_slice_in_dim(group_pad, offset, window, 1)
    query_group = lax.dynamic_slice_in_dim(group_ids, offset, shard_rows, 1)
    query_pos = offset + jnp.arange(shard_rows, dtype=jnp.int32)
    key_pos = offset - HALO + jnp.arange(window, dtype=jnp.int32)
    allowed = build_allowed(query_group, query_pos, key_group, key_pos, lengths)
    scaling = head_dim ** (-0.5)
    scores = jnp.einsum("brhd,bwhd->bhrw", queries, key_rows, preferred_element_type=jnp.float32)
    scores = jnp.where(allowed[:, None], scores * scaling, NEGATIVE)
    row_max = jnp.max(scores, axis=-1, keepdims=True)
    exponent = jnp.exp(scores - row_max)
    probs = exponent / jnp.sum(exponent, axis=-1, keepdims=True)
    probs_low = probs.astype(jnp.bfloat16)
    student_mix = jnp.einsum(
        "bhrw,bwhd->brhd", probs_low, value_rows, preferred_element_type=jnp.float32
    ).astype(jnp.bfloat16)
    mix_flat = student_mix.reshape(dialogs * shard_rows, model_width)
    student_vel = jnp.dot(mix_flat, w_output, preferred_element_type=jnp.float32)
    query_valid = (query_pos[None, :] < lengths[:, None]).reshape(-1)
    difference = jnp.where(query_valid[:, None], student_vel - teacher_vel, 0.0)
    square_local = jnp.sum(difference * difference)
    count_local = jnp.sum(query_valid.astype(jnp.float32))
    grad_vel = difference.astype(jnp.bfloat16)
    grad_mix = jnp.dot(grad_vel, w_output.T, preferred_element_type=jnp.float32).astype(
        jnp.bfloat16
    )
    grad_mix = grad_mix.reshape(dialogs, shard_rows, HEADS, head_dim)
    grad_prob = jnp.einsum(
        "brhd,bwhd->bhrw", grad_mix, value_rows, preferred_element_type=jnp.float32
    )
    grad_score = probs * (grad_prob - jnp.sum(probs * grad_prob, axis=-1, keepdims=True)) * scaling
    grad_score = lax.optimization_barrier(grad_score)
    grad_key = split_product("bhrw,brhd->bwhd", grad_score, queries, True)
    grad_value = jnp.einsum(
        "bhrw,brhd->bwhd", probs_low, grad_mix, preferred_element_type=jnp.float32
    )
    grad_both = jnp.concatenate(
        (
            grad_key.reshape(dialogs, window, model_width),
            grad_value.reshape(dialogs, window, model_width),
        ),
        axis=-1,
    )
    from_next = from_behind(grad_both[:, :HALO].astype(jnp.bfloat16), "seq", -1).astype(jnp.float32)
    from_prev = from_behind(
        grad_both[:, HALO + shard_rows :].astype(jnp.bfloat16), "seq", 1
    ).astype(jnp.float32)
    owned_rows = grad_both[:, HALO : HALO + shard_rows]
    if shard_rows >= 2 * HALO:
        middle = jnp.zeros((dialogs, shard_rows - 2 * HALO, 2 * model_width), jnp.float32)
        owned_rows = owned_rows + jnp.concatenate((from_prev, middle, from_next), axis=1)
    else:
        owned_rows = owned_rows.at[:, :HALO].add(from_prev)
        owned_rows = owned_rows.at[:, shard_rows - HALO :].add(from_next)
    by_head = owned_rows.reshape(shard_rows, 2, HEADS, head_dim).transpose(0, 2, 1, 3)
    head_grads = lax.all_to_all(by_head, "seq", split_axis=1, concat_axis=0, tiled=True)
    head_grads = head_grads.reshape(frames, 2 * head_dim)
    normed_all = lax.all_gather(flat_rows, "seq", axis=0, tiled=True)
    partial = split_product("rf,rg->fg", head_grads, normed_all, False)
    dp_count = lax.axis_size("dp")
    partial = partial.reshape(dp_count, -1)
    lane = jnp.arange(2 * head_dim)
    scalars = jnp.where(lane == 0, square_local, jnp.where(lane == 1, count_local, 0.0))
    partial = jnp.concatenate(
        (partial, jnp.broadcast_to(scalars, (dp_count, 2 * head_dim))), axis=1
    )
    partial = lax.all_to_all(partial, "dp", split_axis=0, concat_axis=0, tiled=True).sum(0)
    block = rows_each * 2 * head_dim
    partial = jnp.concatenate(
        (
            partial[: seq_count * block].reshape(seq_count, block),
            jnp.broadcast_to(partial[seq_count * block :], (seq_count, 2 * head_dim)),
        ),
        axis=1,
    )
    mine = lax.all_to_all(partial, "seq", split_axis=0, concat_axis=0, tiled=True)
    totals = mine[:, block:].sum(0)
    square_sum, frame_count = totals[0], totals[1]
    mean_error = square_sum / (frame_count * model_width)
    mine = mine[:, :block] * lax.rsqrt(frame_count)
    mine = mine.reshape(HEADS, rows_each, 2, head_dim).transpose(2, 1, 0, 3)
    grad_inputs = mine.reshape(2, rows_each, model_width)
    return (grad_inputs, mean_error)


def solution(mesh):
    in_specs = (
        P("dp", "seq", None),
        P("dp", "seq", None),
        P("dp"),
        P("dp", None),
        P("dp"),
        P(),
        P(),
        P(),
        P(None, ("dp", "seq"), None),
        P(("dp", "seq"), None),
    )
    out_specs = (P(None, ("dp", "seq"), None), P())
    return jax.shard_map(shards, mesh=mesh, in_specs=in_specs, out_specs=out_specs, check_vma=False)
```

```python
import jax
import jax.numpy as jnp
from jax import lax
from jax.sharding import PartitionSpec as P

HEADS = 16
HALO = 64
TSTEPS = 1000


EPSILON = 1e-06
NEGATIVE = -1e30


def with_halo(block, sides, width):
    for axis, dim in sides:
        count = lax.axis_size(axis)
        forward = [(i, i + 1) for i in range(count - 1)]
        backward = [(target, source) for source, target in forward]
        low = lax.ppermute(
            lax.slice_in_dim(block, block.shape[dim] - width, None, axis=dim), axis, forward
        )
        high = lax.ppermute(lax.slice_in_dim(block, 0, width, axis=dim), axis, backward)
        block = jnp.concatenate([low, block, high], axis=dim)
    return block


def from_behind(block, axis, distance):
    devices = range(lax.axis_size(axis))
    route = [(i - distance, i) for i in devices if i - distance in devices]
    return lax.ppermute(block, axis, route)


def normalize(clean_frames, noise_frames, time_index, modulation):
    flow_time = (time_index.astype(jnp.float32) + 0.5) / TSTEPS
    flow_time = flow_time[:, None, None]
    blended = (1.0 - flow_time) * noise_frames.astype(
        jnp.float32
    ) + flow_time * clean_frames.astype(jnp.float32)
    inv_rms = lax.rsqrt(jnp.mean(blended * blended, axis=-1, keepdims=True) + EPSILON)
    return (blended * inv_rms * (1.0 + flow_time * modulation)).astype(jnp.bfloat16)


def attend_block(queries, key_rows, values, key_bias):
    scores = jnp.dot(queries, key_rows.T, preferred_element_type=jnp.float32) * queries.shape[
        -1
    ] ** (-0.5)
    scores = scores + key_bias[None, :]
    row_max = jnp.max(scores, axis=-1, keepdims=True)
    exponent = jnp.exp(scores - row_max)
    probs_low = (exponent / jnp.sum(exponent, axis=-1, keepdims=True)).astype(jnp.bfloat16)
    return jnp.dot(probs_low, values, preferred_element_type=jnp.float32).astype(jnp.bfloat16)


def full_attention(queries, key_rows, values, key_bias):
    total_rows = queries.shape[0]
    block_rows = min(512, total_rows)
    blocked = queries.reshape(total_rows // block_rows, block_rows, queries.shape[1])
    result = lax.map(lambda piece: attend_block(piece, key_rows, values, key_bias), blocked)
    return result.reshape(total_rows, values.shape[1])


def teacher_heads(proj_one, bias_one):
    stacked = jnp.transpose(proj_one, (2, 1, 0, 3))
    result = lax.map(
        lambda element: full_attention(element[0], element[1], element[2], bias_one), stacked
    )
    return jnp.transpose(result, (1, 0, 2))


def teacher_direct(proj_one, bias_one):
    def one_head(part):
        return attend_block(part[:, 0], part[:, 1], part[:, 2], bias_one)

    return jax.vmap(one_head, in_axes=2, out_axes=1)(proj_one)


def build_allowed(query_group, query_pos, key_group, key_pos, lengths):
    same_group = key_group[:, None, :] == query_group[:, :, None]
    prev_group = key_group[:, None, :] == query_group[:, :, None] - 1
    live_key = (key_pos[None, :] < lengths[:, None]) & (key_pos[None, :] >= 0)
    itself = key_pos[None, :] == query_pos[:, None]
    return (same_group | prev_group) & (live_key[:, None, :] | itself[None])


def split_product(form, gradient, other, first):
    upper_part = gradient.astype(jnp.bfloat16)
    lower_part = (gradient - upper_part.astype(jnp.float32)).astype(jnp.bfloat16)
    if first:
        return jnp.einsum(form, upper_part, other, preferred_element_type=jnp.float32) + jnp.einsum(
            form, lower_part, other, preferred_element_type=jnp.float32
        )
    return jnp.einsum(form, other, upper_part, preferred_element_type=jnp.float32) + jnp.einsum(
        form, other, lower_part, preferred_element_type=jnp.float32
    )


def shards(
    clean_frames,
    noise_frames,
    lengths,
    group_ids,
    time_index,
    modulation,
    teacher_qkv,
    teacher_out,
    student_in,
    student_out,
):
    dialogs, shard_rows, model_width = clean_frames.shape
    head_dim = model_width // HEADS
    seq_count = lax.axis_size("seq")
    seq_index = lax.axis_index("seq")
    frames = shard_rows * seq_count
    window = shard_rows + 2 * HALO
    rows_each = student_out.shape[0]
    stacked = jnp.concatenate((student_in, student_out[None]), axis=0)
    seq_count = lax.axis_size("seq")
    spread = jnp.broadcast_to(stacked[None], (seq_count,) + stacked.shape)
    spread = lax.all_to_all(spread, "seq", split_axis=0, concat_axis=2, tiled=True)
    gathered = lax.all_gather(spread.reshape(stacked.shape[0], -1, model_width), "dp", axis=1, tiled=True)
    w_inputs = gathered[:3]
    w_output = gathered[3]
    normed = normalize(clean_frames, noise_frames, time_index, modulation)
    flat_rows = normed.reshape(dialogs * shard_rows, model_width)
    normed_all = lax.all_to_all(
        jnp.broadcast_to(flat_rows[None], (seq_count,) + flat_rows.shape),
        "seq",
        split_axis=0,
        concat_axis=0,
        tiled=True,
    ).reshape(-1, model_width)
    frame_pos = jnp.arange(frames, dtype=jnp.int32)
    key_bias = jnp.where(frame_pos[None, :] < lengths[:, None], 0.0, NEGATIVE).astype(jnp.float32)
    teacher_proj = jnp.dot(flat_rows, teacher_qkv, preferred_element_type=jnp.float32).astype(
        jnp.bfloat16
    )
    teacher_proj = teacher_proj.reshape(dialogs, shard_rows, 3, HEADS, head_dim)
    by_heads = lax.all_to_all(teacher_proj, "seq", split_axis=3, concat_axis=1, tiled=True)
    head_out = jax.vmap(teacher_direct)(by_heads, key_bias)
    heads_here = head_out.shape[2]
    head_out = head_out.reshape(dialogs, seq_count, shard_rows, heads_here, head_dim)
    by_frames = lax.all_to_all(head_out, "seq", split_axis=1, concat_axis=1, tiled=True)
    teacher_vel = jnp.einsum(
        "bsfhd,shdn->bfn",
        by_frames,
        teacher_out.reshape(seq_count, heads_here, head_dim, model_width),
        preferred_element_type=jnp.float32,
    ).reshape(dialogs * shard_rows, model_width)
    offset = seq_index * shard_rows
    queries = jnp.dot(flat_rows, w_inputs[0], preferred_element_type=jnp.float32).astype(
        jnp.bfloat16
    )
    queries = queries.reshape(dialogs, shard_rows, HEADS, head_dim)
    key_local = jnp.dot(flat_rows, w_inputs[1], preferred_element_type=jnp.float32).astype(
        jnp.bfloat16
    )
    value_local = jnp.dot(flat_rows, w_inputs[2], preferred_element_type=jnp.float32).astype(
        jnp.bfloat16
    )
    both_local = jnp.concatenate((key_local, value_local), axis=-1).reshape(
        dialogs, shard_rows, 2 * model_width
    )
    both_window = with_halo(both_local, (("seq", 1),), HALO)
    key_rows = both_window[:, :, :model_width].reshape(dialogs, window, HEADS, head_dim)
    value_rows = both_window[:, :, model_width:].reshape(dialogs, window, HEADS, head_dim)
    group_pad = jnp.pad(group_ids, ((0, 0), (HALO, HALO)), constant_values=-10)
    key_group = lax.dynamic_slice_in_dim(group_pad, offset, window, 1)
    query_group = lax.dynamic_slice_in_dim(group_ids, offset, shard_rows, 1)
    query_pos = offset + jnp.arange(shard_rows, dtype=jnp.int32)
    key_pos = offset - HALO + jnp.arange(window, dtype=jnp.int32)
    allowed = build_allowed(query_group, query_pos, key_group, key_pos, lengths)
    scaling = head_dim ** (-0.5)
    scores = jnp.einsum("brhd,bwhd->bhrw", queries, key_rows, preferred_element_type=jnp.float32)
    scores = jnp.where(allowed[:, None], scores * scaling, NEGATIVE)
    row_max = jnp.max(scores, axis=-1, keepdims=True)
    exponent = jnp.exp(scores - row_max)
    probs = exponent / jnp.sum(exponent, axis=-1, keepdims=True)
    probs_low = probs.astype(jnp.bfloat16)
    student_mix = jnp.einsum(
        "bhrw,bwhd->brhd", probs_low, value_rows, preferred_element_type=jnp.float32
    ).astype(jnp.bfloat16)
    mix_flat = student_mix.reshape(dialogs * shard_rows, model_width)
    student_vel = jnp.dot(mix_flat, w_output, preferred_element_type=jnp.float32)
    query_valid = (query_pos[None, :] < lengths[:, None]).reshape(-1)
    difference = jnp.where(query_valid[:, None], student_vel - teacher_vel, 0.0)
    square_local = jnp.sum(difference * difference)
    count_local = jnp.sum(query_valid.astype(jnp.float32))
    grad_vel = difference.astype(jnp.bfloat16)
    grad_mix = jnp.dot(grad_vel, w_output.T, preferred_element_type=jnp.float32).astype(
        jnp.bfloat16
    )
    grad_mix = grad_mix.reshape(dialogs, shard_rows, HEADS, head_dim)
    grad_prob = jnp.einsum(
        "brhd,bwhd->bhrw", grad_mix, value_rows, preferred_element_type=jnp.float32
    )
    grad_score = probs * (grad_prob - jnp.sum(probs * grad_prob, axis=-1, keepdims=True)) * scaling
    grad_score = lax.optimization_barrier(grad_score)
    grad_key = split_product("bhrw,brhd->bwhd", grad_score, queries, True)
    grad_value = jnp.einsum(
        "bhrw,brhd->bwhd", probs_low, grad_mix, preferred_element_type=jnp.float32
    )
    grad_both = jnp.concatenate(
        (
            grad_key.reshape(dialogs, window, model_width),
            grad_value.reshape(dialogs, window, model_width),
        ),
        axis=-1,
    )
    from_next = from_behind(grad_both[:, :HALO].astype(jnp.bfloat16), "seq", -1).astype(jnp.float32)
    from_prev = from_behind(
        grad_both[:, HALO + shard_rows :].astype(jnp.bfloat16), "seq", 1
    ).astype(jnp.float32)
    owned_rows = grad_both[:, HALO : HALO + shard_rows]
    if shard_rows >= 2 * HALO:
        middle = jnp.zeros((dialogs, shard_rows - 2 * HALO, 2 * model_width), jnp.float32)
        owned_rows = owned_rows + jnp.concatenate((from_prev, middle, from_next), axis=1)
    else:
        owned_rows = owned_rows.at[:, :HALO].add(from_prev)
        owned_rows = owned_rows.at[:, shard_rows - HALO :].add(from_next)
    by_head = owned_rows.reshape(shard_rows, 2, HEADS, head_dim).transpose(0, 2, 1, 3)
    head_grads = lax.all_to_all(by_head, "seq", split_axis=1, concat_axis=0, tiled=True)
    head_grads = head_grads.reshape(frames, 2 * head_dim)
    partial = split_product("rf,rg->fg", head_grads, normed_all, False)
    dp_count = lax.axis_size("dp")
    block = rows_each * 2 * head_dim
    partial = partial.reshape(dp_count * seq_count, block)
    lane = jnp.arange(2 * head_dim)
    scalars = jnp.where(lane == 0, square_local, jnp.where(lane == 1, count_local, 0.0))
    partial = jnp.concatenate(
        (partial, jnp.broadcast_to(scalars, (dp_count * seq_count, 2 * head_dim))), axis=1
    )
    mine = lax.all_to_all(partial, ("dp", "seq"), split_axis=0, concat_axis=0, tiled=True)
    mine = mine.reshape(dp_count, seq_count, block + 2 * head_dim)
    totals = mine[:, :, block:].sum((0, 1))
    square_sum, frame_count = totals[0], totals[1]
    mean_error = square_sum / (frame_count * model_width)
    mine = mine[:, :, :block].sum(0) * lax.rsqrt(frame_count)
    mine = mine.reshape(HEADS, rows_each, 2, head_dim).transpose(2, 1, 0, 3)
    grad_inputs = mine.reshape(2, rows_each, model_width)
    return (grad_inputs, mean_error)


def solution(mesh):
    in_specs = (
        P("dp", "seq", None),
        P("dp", "seq", None),
        P("dp"),
        P("dp", None),
        P("dp"),
        P(),
        P(),
        P(),
        P(None, ("dp", "seq"), None),
        P(("dp", "seq"), None),
    )
    out_specs = (P(None, ("dp", "seq"), None), P())
    return jax.shard_map(shards, mesh=mesh, in_specs=in_specs, out_specs=out_specs, check_vma=False)
```

```python
import jax
import jax.numpy as jnp
from jax import lax
from jax.sharding import PartitionSpec as P

HEADS = 16
HALO = 64
TSTEPS = 1000


EPSILON = 1e-06
NEGATIVE = -1e30


def with_halo(block, sides, width):
    for axis, dim in sides:
        count = lax.axis_size(axis)
        forward = [(i, i + 1) for i in range(count - 1)]
        backward = [(target, source) for source, target in forward]
        low = lax.ppermute(
            lax.slice_in_dim(block, block.shape[dim] - width, None, axis=dim), axis, forward
        )
        high = lax.ppermute(lax.slice_in_dim(block, 0, width, axis=dim), axis, backward)
        block = jnp.concatenate([low, block, high], axis=dim)
    return block


def from_behind(block, axis, distance):
    devices = range(lax.axis_size(axis))
    route = [(i - distance, i) for i in devices if i - distance in devices]
    return lax.ppermute(block, axis, route)


def normalize(clean_frames, noise_frames, time_index, modulation):
    flow_time = (time_index.astype(jnp.float32) + 0.5) / TSTEPS
    flow_time = flow_time[:, None, None]
    blended = (1.0 - flow_time) * noise_frames.astype(
        jnp.float32
    ) + flow_time * clean_frames.astype(jnp.float32)
    inv_rms = lax.rsqrt(jnp.mean(blended * blended, axis=-1, keepdims=True) + EPSILON)
    return (blended * inv_rms * (1.0 + flow_time * modulation)).astype(jnp.bfloat16)


def attend_block(queries, key_rows, values, key_bias):
    scores = jnp.dot(queries, key_rows.T, preferred_element_type=jnp.float32) * queries.shape[
        -1
    ] ** (-0.5)
    scores = scores + key_bias[None, :]
    row_max = jnp.max(scores, axis=-1, keepdims=True)
    exponent = jnp.exp(scores - row_max)
    probs_low = (exponent / jnp.sum(exponent, axis=-1, keepdims=True)).astype(jnp.bfloat16)
    return jnp.dot(probs_low, values, preferred_element_type=jnp.float32).astype(jnp.bfloat16)


def full_attention(queries, key_rows, values, key_bias):
    total_rows = queries.shape[0]
    block_rows = min(512, total_rows)
    blocked = queries.reshape(total_rows // block_rows, block_rows, queries.shape[1])
    result = lax.map(lambda piece: attend_block(piece, key_rows, values, key_bias), blocked)
    return result.reshape(total_rows, values.shape[1])


def teacher_heads(proj_one, bias_one):
    stacked = jnp.transpose(proj_one, (2, 1, 0, 3))
    result = lax.map(
        lambda element: full_attention(element[0], element[1], element[2], bias_one), stacked
    )
    return jnp.transpose(result, (1, 0, 2))


def teacher_direct(proj_one, bias_one):
    def one_head(part):
        return attend_block(part[:, 0], part[:, 1], part[:, 2], bias_one)

    return jax.vmap(one_head, in_axes=2, out_axes=1)(proj_one)


def build_allowed(query_group, query_pos, key_group, key_pos, lengths):
    same_group = key_group[:, None, :] == query_group[:, :, None]
    prev_group = key_group[:, None, :] == query_group[:, :, None] - 1
    live_key = (key_pos[None, :] < lengths[:, None]) & (key_pos[None, :] >= 0)
    itself = key_pos[None, :] == query_pos[:, None]
    return (same_group | prev_group) & (live_key[:, None, :] | itself[None])


def split_product(form, gradient, other, first):
    upper_part = gradient.astype(jnp.bfloat16)
    lower_part = (gradient - upper_part.astype(jnp.float32)).astype(jnp.bfloat16)
    if first:
        return jnp.einsum(form, upper_part, other, preferred_element_type=jnp.float32) + jnp.einsum(
            form, lower_part, other, preferred_element_type=jnp.float32
        )
    return jnp.einsum(form, other, upper_part, preferred_element_type=jnp.float32) + jnp.einsum(
        form, other, lower_part, preferred_element_type=jnp.float32
    )


def shards(
    clean_frames,
    noise_frames,
    lengths,
    group_ids,
    time_index,
    modulation,
    teacher_qkv,
    teacher_out,
    student_in,
    student_out,
):
    dialogs, shard_rows, model_width = clean_frames.shape
    head_dim = model_width // HEADS
    seq_count = lax.axis_size("seq")
    seq_index = lax.axis_index("seq")
    frames = shard_rows * seq_count
    window = shard_rows + 2 * HALO
    rows_each = student_out.shape[0]
    stacked = jnp.concatenate((student_in, student_out[None]), axis=0)
    gathered = lax.all_gather(
        lax.all_gather(stacked, "seq", axis=1, tiled=True), "dp", axis=1, tiled=True
    )
    w_inputs = gathered[:3]
    w_output = gathered[3]
    normed = normalize(clean_frames, noise_frames, time_index, modulation)
    flat_rows = normed.reshape(dialogs * shard_rows, model_width)
    frame_pos = jnp.arange(frames, dtype=jnp.int32)
    key_bias = jnp.where(frame_pos[None, :] < lengths[:, None], 0.0, NEGATIVE).astype(jnp.float32)
    teacher_proj = jnp.dot(flat_rows, teacher_qkv, preferred_element_type=jnp.float32).astype(
        jnp.bfloat16
    )
    teacher_proj = teacher_proj.reshape(dialogs, shard_rows, 3, HEADS, head_dim)
    by_heads = lax.all_to_all(teacher_proj, "seq", split_axis=3, concat_axis=1, tiled=True)
    head_out = jax.vmap(teacher_direct)(by_heads, key_bias)
    heads_here = head_out.shape[2]
    head_out = head_out.reshape(dialogs, seq_count, shard_rows, heads_here, head_dim)
    by_frames = lax.all_to_all(head_out, "seq", split_axis=1, concat_axis=1, tiled=True)
    teacher_vel = jnp.einsum(
        "bsfhd,shdn->bfn",
        by_frames,
        teacher_out.reshape(seq_count, heads_here, head_dim, model_width),
        preferred_element_type=jnp.float32,
    ).reshape(dialogs * shard_rows, model_width)
    offset = seq_index * shard_rows
    queries = jnp.dot(flat_rows, w_inputs[0], preferred_element_type=jnp.float32).astype(
        jnp.bfloat16
    )
    queries = queries.reshape(dialogs, shard_rows, HEADS, head_dim)
    key_local = jnp.dot(flat_rows, w_inputs[1], preferred_element_type=jnp.float32).astype(
        jnp.bfloat16
    )
    value_local = jnp.dot(flat_rows, w_inputs[2], preferred_element_type=jnp.float32).astype(
        jnp.bfloat16
    )
    both_local = jnp.concatenate((key_local, value_local), axis=-1).reshape(
        dialogs, shard_rows, 2 * model_width
    )
    both_window = with_halo(both_local, (("seq", 1),), HALO)
    key_rows = both_window[:, :, :model_width].reshape(dialogs, window, HEADS, head_dim)
    value_rows = both_window[:, :, model_width:].reshape(dialogs, window, HEADS, head_dim)
    group_pad = jnp.pad(group_ids, ((0, 0), (HALO, HALO)), constant_values=-10)
    key_group = lax.dynamic_slice_in_dim(group_pad, offset, window, 1)
    query_group = lax.dynamic_slice_in_dim(group_ids, offset, shard_rows, 1)
    query_pos = offset + jnp.arange(shard_rows, dtype=jnp.int32)
    key_pos = offset - HALO + jnp.arange(window, dtype=jnp.int32)
    allowed = build_allowed(query_group, query_pos, key_group, key_pos, lengths)
    scaling = head_dim ** (-0.5)
    scores = jnp.einsum("brhd,bwhd->bhrw", queries, key_rows, preferred_element_type=jnp.float32)
    scores = jnp.where(allowed[:, None], scores * scaling, NEGATIVE)
    row_max = jnp.max(scores, axis=-1, keepdims=True)
    exponent = jnp.exp(scores - row_max)
    probs = exponent / jnp.sum(exponent, axis=-1, keepdims=True)
    probs_low = probs.astype(jnp.bfloat16)
    student_mix = jnp.einsum(
        "bhrw,bwhd->brhd", probs_low, value_rows, preferred_element_type=jnp.float32
    ).astype(jnp.bfloat16)
    mix_flat = student_mix.reshape(dialogs * shard_rows, model_width)
    student_vel = jnp.dot(mix_flat, w_output, preferred_element_type=jnp.float32)
    query_valid = (query_pos[None, :] < lengths[:, None]).reshape(-1)
    difference = jnp.where(query_valid[:, None], student_vel - teacher_vel, 0.0)
    square_local = jnp.sum(difference * difference)
    count_local = jnp.sum(query_valid.astype(jnp.float32))
    grad_vel = difference.astype(jnp.bfloat16)
    grad_mix = jnp.dot(grad_vel, w_output.T, preferred_element_type=jnp.float32).astype(
        jnp.bfloat16
    )
    grad_mix = grad_mix.reshape(dialogs, shard_rows, HEADS, head_dim)
    grad_prob = jnp.einsum(
        "brhd,bwhd->bhrw", grad_mix, value_rows, preferred_element_type=jnp.float32
    )
    grad_score = probs * (grad_prob - jnp.sum(probs * grad_prob, axis=-1, keepdims=True)) * scaling
    grad_score = lax.optimization_barrier(grad_score)
    grad_key = split_product("bhrw,brhd->bwhd", grad_score, queries, True)
    grad_value = jnp.einsum(
        "bhrw,brhd->bwhd", probs_low, grad_mix, preferred_element_type=jnp.float32
    )
    grad_both = jnp.concatenate(
        (
            grad_key.reshape(dialogs, window, model_width),
            grad_value.reshape(dialogs, window, model_width),
        ),
        axis=-1,
    )
    from_next = from_behind(grad_both[:, :HALO].astype(jnp.bfloat16), "seq", -1).astype(jnp.float32)
    from_prev = from_behind(
        grad_both[:, HALO + shard_rows :].astype(jnp.bfloat16), "seq", 1
    ).astype(jnp.float32)
    owned_rows = grad_both[:, HALO : HALO + shard_rows]
    if shard_rows >= 2 * HALO:
        middle = jnp.zeros((dialogs, shard_rows - 2 * HALO, 2 * model_width), jnp.float32)
        owned_rows = owned_rows + jnp.concatenate((from_prev, middle, from_next), axis=1)
    else:
        owned_rows = owned_rows.at[:, :HALO].add(from_prev)
        owned_rows = owned_rows.at[:, shard_rows - HALO :].add(from_next)
    by_head = owned_rows.reshape(shard_rows, 2, HEADS, head_dim).transpose(0, 2, 1, 3)
    head_grads = lax.all_to_all(
        by_head.astype(jnp.bfloat16), "seq", split_axis=1, concat_axis=0, tiled=True
    )
    head_grads = head_grads.reshape(frames, 2 * head_dim)
    normed_all = lax.all_gather(flat_rows, "seq", axis=0, tiled=True)
    partial = jnp.dot(normed_all.T, head_grads, preferred_element_type=jnp.float32)
    dp_count = lax.axis_size("dp")
    block = rows_each * 2 * head_dim
    partial = partial.reshape(dp_count * seq_count, block)
    lane = jnp.arange(2 * head_dim)
    scalars = jnp.where(lane == 0, square_local, jnp.where(lane == 1, count_local, 0.0))
    partial = jnp.concatenate(
        (partial, jnp.broadcast_to(scalars, (dp_count * seq_count, 2 * head_dim))), axis=1
    )
    mine = lax.all_to_all(partial, ("dp", "seq"), split_axis=0, concat_axis=0, tiled=True)
    mine = mine.reshape(dp_count, seq_count, block + 2 * head_dim)
    totals = mine[:, :, block:].sum((0, 1))
    square_sum, frame_count = totals[0], totals[1]
    mean_error = square_sum / (frame_count * model_width)
    mine = mine[:, :, :block].sum(0) * lax.rsqrt(frame_count)
    mine = mine.reshape(HEADS, rows_each, 2, head_dim).transpose(2, 1, 0, 3)
    grad_inputs = mine.reshape(2, rows_each, model_width)
    return (grad_inputs, mean_error)


def solution(mesh):
    in_specs = (
        P("dp", "seq", None),
        P("dp", "seq", None),
        P("dp"),
        P("dp", None),
        P("dp"),
        P(),
        P(),
        P(),
        P(None, ("dp", "seq"), None),
        P(("dp", "seq"), None),
    )
    out_specs = (P(None, ("dp", "seq"), None), P())
    return jax.shard_map(shards, mesh=mesh, in_specs=in_specs, out_specs=out_specs, check_vma=False)
```

```python
import jax
import jax.numpy as jnp
from jax import lax
from jax.sharding import PartitionSpec as P

HEADS = 16
HALO = 64
TSTEPS = 1000


EPSILON = 1e-06
NEGATIVE = -1e30


def with_halo(block, sides, width):
    for axis, dim in sides:
        count = lax.axis_size(axis)
        forward = [(i, i + 1) for i in range(count - 1)]
        backward = [(target, source) for source, target in forward]
        low = lax.ppermute(
            lax.slice_in_dim(block, block.shape[dim] - width, None, axis=dim), axis, forward
        )
        high = lax.ppermute(lax.slice_in_dim(block, 0, width, axis=dim), axis, backward)
        block = jnp.concatenate([low, block, high], axis=dim)
    return block


def from_behind(block, axis, distance):
    devices = range(lax.axis_size(axis))
    route = [(i - distance, i) for i in devices if i - distance in devices]
    return lax.ppermute(block, axis, route)


def normalize(clean_frames, noise_frames, time_index, modulation):
    flow_time = (time_index.astype(jnp.float32) + 0.5) / TSTEPS
    flow_time = flow_time[:, None, None]
    blended = (1.0 - flow_time) * noise_frames.astype(
        jnp.float32
    ) + flow_time * clean_frames.astype(jnp.float32)
    inv_rms = lax.rsqrt(jnp.mean(blended * blended, axis=-1, keepdims=True) + EPSILON)
    return (blended * inv_rms * (1.0 + flow_time * modulation)).astype(jnp.bfloat16)


def attend_block(queries, key_rows, values, key_bias):
    scores = jnp.dot(queries, key_rows.T, preferred_element_type=jnp.float32) * queries.shape[
        -1
    ] ** (-0.5)
    scores = scores + key_bias[None, :]
    row_max = jnp.max(scores, axis=-1, keepdims=True)
    exponent = jnp.exp(scores - row_max)
    probs_low = (exponent / jnp.sum(exponent, axis=-1, keepdims=True)).astype(jnp.bfloat16)
    return jnp.dot(probs_low, values, preferred_element_type=jnp.float32).astype(jnp.bfloat16)


def full_attention(queries, key_rows, values, key_bias):
    total_rows = queries.shape[0]
    block_rows = min(512, total_rows)
    blocked = queries.reshape(total_rows // block_rows, block_rows, queries.shape[1])
    result = lax.map(lambda piece: attend_block(piece, key_rows, values, key_bias), blocked)
    return result.reshape(total_rows, values.shape[1])


def teacher_heads(proj_one, bias_one):
    stacked = jnp.transpose(proj_one, (2, 1, 0, 3))
    result = lax.map(
        lambda element: full_attention(element[0], element[1], element[2], bias_one), stacked
    )
    return jnp.transpose(result, (1, 0, 2))


def teacher_direct(proj_one, bias_one):
    def one_head(part):
        return attend_block(part[:, 0], part[:, 1], part[:, 2], bias_one)

    return jax.vmap(one_head, in_axes=2, out_axes=1)(proj_one)


def build_allowed(query_group, query_pos, key_group, key_pos, lengths):
    same_group = key_group[:, None, :] == query_group[:, :, None]
    prev_group = key_group[:, None, :] == query_group[:, :, None] - 1
    live_key = (key_pos[None, :] < lengths[:, None]) & (key_pos[None, :] >= 0)
    itself = key_pos[None, :] == query_pos[:, None]
    return (same_group | prev_group) & (live_key[:, None, :] | itself[None])


def split_product(form, gradient, other, first):
    upper_part = gradient.astype(jnp.bfloat16)
    lower_part = (gradient - upper_part.astype(jnp.float32)).astype(jnp.bfloat16)
    if first:
        return jnp.einsum(form, upper_part, other, preferred_element_type=jnp.float32) + jnp.einsum(
            form, lower_part, other, preferred_element_type=jnp.float32
        )
    return jnp.einsum(form, other, upper_part, preferred_element_type=jnp.float32) + jnp.einsum(
        form, other, lower_part, preferred_element_type=jnp.float32
    )


def shards(
    clean_frames,
    noise_frames,
    lengths,
    group_ids,
    time_index,
    modulation,
    teacher_qkv,
    teacher_out,
    student_in,
    student_out,
):
    dialogs, shard_rows, model_width = clean_frames.shape
    head_dim = model_width // HEADS
    seq_count = lax.axis_size("seq")
    seq_index = lax.axis_index("seq")
    frames = shard_rows * seq_count
    window = shard_rows + 2 * HALO
    rows_each = student_out.shape[0]
    stacked = jnp.concatenate((student_in, student_out[None]), axis=0)
    by_seq = lax.all_gather(stacked, "seq", axis=1, tiled=True)
    w_inputs = lax.all_gather(by_seq[:3], "dp", axis=1, tiled=True)
    w_output = lax.all_gather(by_seq[3], "dp", axis=0, tiled=True)
    normed = normalize(clean_frames, noise_frames, time_index, modulation)
    flat_rows = normed.reshape(dialogs * shard_rows, model_width)
    frame_pos = jnp.arange(frames, dtype=jnp.int32)
    key_bias = jnp.where(frame_pos[None, :] < lengths[:, None], 0.0, NEGATIVE).astype(jnp.float32)
    teacher_proj = jnp.dot(flat_rows, teacher_qkv, preferred_element_type=jnp.float32).astype(
        jnp.bfloat16
    )
    teacher_proj = teacher_proj.reshape(dialogs, shard_rows, 3, HEADS, head_dim)
    by_heads = lax.all_to_all(teacher_proj, "seq", split_axis=3, concat_axis=1, tiled=True)
    head_out = jax.vmap(teacher_direct)(by_heads, key_bias)
    heads_here = head_out.shape[2]
    head_out = head_out.reshape(dialogs, seq_count, shard_rows, heads_here, head_dim)
    by_frames = lax.all_to_all(head_out, "seq", split_axis=1, concat_axis=1, tiled=True)
    teacher_vel = jnp.einsum(
        "bsfhd,shdn->bfn",
        by_frames,
        teacher_out.reshape(seq_count, heads_here, head_dim, model_width),
        preferred_element_type=jnp.float32,
    ).reshape(dialogs * shard_rows, model_width)
    offset = seq_index * shard_rows
    queries = jnp.dot(flat_rows, w_inputs[0], preferred_element_type=jnp.float32).astype(
        jnp.bfloat16
    )
    queries = queries.reshape(dialogs, shard_rows, HEADS, head_dim)
    key_local = jnp.dot(flat_rows, w_inputs[1], preferred_element_type=jnp.float32).astype(
        jnp.bfloat16
    )
    value_local = jnp.dot(flat_rows, w_inputs[2], preferred_element_type=jnp.float32).astype(
        jnp.bfloat16
    )
    both_local = jnp.concatenate((key_local, value_local), axis=-1).reshape(
        dialogs, shard_rows, 2 * model_width
    )
    both_window = with_halo(both_local, (("seq", 1),), HALO)
    key_rows = both_window[:, :, :model_width].reshape(dialogs, window, HEADS, head_dim)
    value_rows = both_window[:, :, model_width:].reshape(dialogs, window, HEADS, head_dim)
    group_pad = jnp.pad(group_ids, ((0, 0), (HALO, HALO)), constant_values=-10)
    key_group = lax.dynamic_slice_in_dim(group_pad, offset, window, 1)
    query_group = lax.dynamic_slice_in_dim(group_ids, offset, shard_rows, 1)
    query_pos = offset + jnp.arange(shard_rows, dtype=jnp.int32)
    key_pos = offset - HALO + jnp.arange(window, dtype=jnp.int32)
    allowed = build_allowed(query_group, query_pos, key_group, key_pos, lengths)
    scaling = head_dim ** (-0.5)
    scores = jnp.einsum("brhd,bwhd->bhrw", queries, key_rows, preferred_element_type=jnp.float32)
    scores = jnp.where(allowed[:, None], scores * scaling, NEGATIVE)
    row_max = jnp.max(scores, axis=-1, keepdims=True)
    exponent = jnp.exp(scores - row_max)
    probs = exponent / jnp.sum(exponent, axis=-1, keepdims=True)
    probs_low = probs.astype(jnp.bfloat16)
    student_mix = jnp.einsum(
        "bhrw,bwhd->brhd", probs_low, value_rows, preferred_element_type=jnp.float32
    ).astype(jnp.bfloat16)
    mix_flat = student_mix.reshape(dialogs * shard_rows, model_width)
    student_vel = jnp.dot(mix_flat, w_output, preferred_element_type=jnp.float32)
    query_valid = (query_pos[None, :] < lengths[:, None]).reshape(-1)
    difference = jnp.where(query_valid[:, None], student_vel - teacher_vel, 0.0)
    square_local = jnp.sum(difference * difference)
    count_local = jnp.sum(query_valid.astype(jnp.float32))
    grad_vel = difference.astype(jnp.bfloat16)
    grad_mix = jnp.dot(grad_vel, w_output.T, preferred_element_type=jnp.float32).astype(
        jnp.bfloat16
    )
    grad_mix = grad_mix.reshape(dialogs, shard_rows, HEADS, head_dim)
    grad_prob = jnp.einsum(
        "brhd,bwhd->bhrw", grad_mix, value_rows, preferred_element_type=jnp.float32
    )
    grad_score = probs * (grad_prob - jnp.sum(probs * grad_prob, axis=-1, keepdims=True)) * scaling
    grad_score = lax.optimization_barrier(grad_score)
    grad_key = split_product("bhrw,brhd->bwhd", grad_score, queries, True)
    grad_value = jnp.einsum(
        "bhrw,brhd->bwhd", probs_low, grad_mix, preferred_element_type=jnp.float32
    )
    grad_both = jnp.concatenate(
        (
            grad_key.reshape(dialogs, window, model_width),
            grad_value.reshape(dialogs, window, model_width),
        ),
        axis=-1,
    )
    from_next = from_behind(grad_both[:, :HALO].astype(jnp.bfloat16), "seq", -1).astype(jnp.float32)
    from_prev = from_behind(
        grad_both[:, HALO + shard_rows :].astype(jnp.bfloat16), "seq", 1
    ).astype(jnp.float32)
    owned_rows = grad_both[:, HALO : HALO + shard_rows]
    if shard_rows >= 2 * HALO:
        middle = jnp.zeros((dialogs, shard_rows - 2 * HALO, 2 * model_width), jnp.float32)
        owned_rows = owned_rows + jnp.concatenate((from_prev, middle, from_next), axis=1)
    else:
        owned_rows = owned_rows.at[:, :HALO].add(from_prev)
        owned_rows = owned_rows.at[:, shard_rows - HALO :].add(from_next)
    by_head = owned_rows.reshape(shard_rows, 2, HEADS, head_dim).transpose(0, 2, 1, 3)
    head_grads = lax.all_to_all(
        by_head.astype(jnp.bfloat16), "seq", split_axis=1, concat_axis=0, tiled=True
    )
    head_grads = head_grads.reshape(frames, 2 * head_dim)
    normed_all = lax.all_gather(flat_rows, "seq", axis=0, tiled=True)
    partial = jnp.dot(normed_all.T, head_grads, preferred_element_type=jnp.float32)
    dp_count = lax.axis_size("dp")
    block = rows_each * 2 * head_dim
    partial = partial.reshape(dp_count * seq_count, block)
    lane = jnp.arange(2 * head_dim)
    scalars = jnp.where(lane == 0, square_local, jnp.where(lane == 1, count_local, 0.0))
    partial = jnp.concatenate(
        (partial, jnp.broadcast_to(scalars, (dp_count * seq_count, 2 * head_dim))), axis=1
    )
    mine = lax.all_to_all(partial, ("dp", "seq"), split_axis=0, concat_axis=0, tiled=True)
    mine = mine.reshape(dp_count, seq_count, block + 2 * head_dim)
    totals = mine[:, :, block:].sum((0, 1))
    square_sum, frame_count = totals[0], totals[1]
    mean_error = square_sum / (frame_count * model_width)
    mine = mine[:, :, :block].sum(0) * lax.rsqrt(frame_count)
    mine = mine.reshape(HEADS, rows_each, 2, head_dim).transpose(2, 1, 0, 3)
    grad_inputs = mine.reshape(2, rows_each, model_width)
    return (grad_inputs, mean_error)


def solution(mesh):
    in_specs = (
        P("dp", "seq", None),
        P("dp", "seq", None),
        P("dp"),
        P("dp", None),
        P("dp"),
        P(),
        P(),
        P(),
        P(None, ("dp", "seq"), None),
        P(("dp", "seq"), None),
    )
    out_specs = (P(None, ("dp", "seq"), None), P())
    return jax.shard_map(shards, mesh=mesh, in_specs=in_specs, out_specs=out_specs, check_vma=False)
```

```python
import jax
import jax.numpy as jnp
from jax import lax
from jax.sharding import PartitionSpec as P

HEADS = 16
HALO = 64
TSTEPS = 1000


EPSILON = 1e-06
NEGATIVE = -1e30


def with_halo(block, sides, width):
    for axis, dim in sides:
        count = lax.axis_size(axis)
        forward = [(i, i + 1) for i in range(count - 1)]
        backward = [(target, source) for source, target in forward]
        low = lax.ppermute(
            lax.slice_in_dim(block, block.shape[dim] - width, None, axis=dim), axis, forward
        )
        high = lax.ppermute(lax.slice_in_dim(block, 0, width, axis=dim), axis, backward)
        block = jnp.concatenate([low, block, high], axis=dim)
    return block


def from_behind(block, axis, distance):
    devices = range(lax.axis_size(axis))
    route = [(i - distance, i) for i in devices if i - distance in devices]
    return lax.ppermute(block, axis, route)


def normalize(clean_frames, noise_frames, time_index, modulation):
    flow_time = (time_index.astype(jnp.float32) + 0.5) / TSTEPS
    flow_time = flow_time[:, None, None]
    blended = (1.0 - flow_time) * noise_frames.astype(
        jnp.float32
    ) + flow_time * clean_frames.astype(jnp.float32)
    inv_rms = lax.rsqrt(jnp.mean(blended * blended, axis=-1, keepdims=True) + EPSILON)
    return (blended * inv_rms * (1.0 + flow_time * modulation)).astype(jnp.bfloat16)


def attend_block(queries, key_rows, values, key_bias):
    scores = jnp.dot(queries, key_rows.T, preferred_element_type=jnp.float32) * queries.shape[
        -1
    ] ** (-0.5)
    scores = scores + key_bias[None, :]
    row_max = jnp.max(scores, axis=-1, keepdims=True)
    exponent = jnp.exp(scores - row_max)
    probs_low = (exponent / jnp.sum(exponent, axis=-1, keepdims=True)).astype(jnp.bfloat16)
    return jnp.dot(probs_low, values, preferred_element_type=jnp.float32).astype(jnp.bfloat16)


def full_attention(queries, key_rows, values, key_bias):
    total_rows = queries.shape[0]
    block_rows = min(512, total_rows)
    blocked = queries.reshape(total_rows // block_rows, block_rows, queries.shape[1])
    result = lax.map(lambda piece: attend_block(piece, key_rows, values, key_bias), blocked)
    return result.reshape(total_rows, values.shape[1])


def teacher_heads(proj_one, bias_one):
    stacked = jnp.transpose(proj_one, (2, 1, 0, 3))
    result = lax.map(
        lambda element: full_attention(element[0], element[1], element[2], bias_one), stacked
    )
    return jnp.transpose(result, (1, 0, 2))


def teacher_direct(proj_one, bias_one):
    def one_head(part):
        return attend_block(part[:, 0], part[:, 1], part[:, 2], bias_one)

    return jax.vmap(one_head, in_axes=2, out_axes=1)(proj_one)


def build_allowed(query_group, query_pos, key_group, key_pos, lengths):
    same_group = key_group[:, None, :] == query_group[:, :, None]
    prev_group = key_group[:, None, :] == query_group[:, :, None] - 1
    live_key = (key_pos[None, :] < lengths[:, None]) & (key_pos[None, :] >= 0)
    itself = key_pos[None, :] == query_pos[:, None]
    return (same_group | prev_group) & (live_key[:, None, :] | itself[None])


def split_product(form, gradient, other, first):
    upper_part = gradient.astype(jnp.bfloat16)
    lower_part = (gradient - upper_part.astype(jnp.float32)).astype(jnp.bfloat16)
    if first:
        return jnp.einsum(form, upper_part, other, preferred_element_type=jnp.float32) + jnp.einsum(
            form, lower_part, other, preferred_element_type=jnp.float32
        )
    return jnp.einsum(form, other, upper_part, preferred_element_type=jnp.float32) + jnp.einsum(
        form, other, lower_part, preferred_element_type=jnp.float32
    )


def shards(
    clean_frames,
    noise_frames,
    lengths,
    group_ids,
    time_index,
    modulation,
    teacher_qkv,
    teacher_out,
    student_in,
    student_out,
):
    dialogs, shard_rows, model_width = clean_frames.shape
    head_dim = model_width // HEADS
    seq_count = lax.axis_size("seq")
    seq_index = lax.axis_index("seq")
    frames = shard_rows * seq_count
    window = shard_rows + 2 * HALO
    rows_each = student_out.shape[0]
    stacked = jnp.concatenate((student_in, student_out[None]), axis=0)
    gathered = lax.all_gather(
        lax.all_gather(stacked, "seq", axis=1, tiled=True), "dp", axis=1, tiled=True
    )
    w_inputs = gathered[:3]
    w_output = gathered[3]
    normed = normalize(clean_frames, noise_frames, time_index, modulation)
    flat_rows = normed.reshape(dialogs * shard_rows, model_width)
    frame_pos = jnp.arange(frames, dtype=jnp.int32)
    key_bias = jnp.where(frame_pos[None, :] < lengths[:, None], 0.0, NEGATIVE).astype(jnp.float32)
    teacher_proj = jnp.dot(flat_rows, teacher_qkv, preferred_element_type=jnp.float32).astype(
        jnp.bfloat16
    )
    teacher_proj = teacher_proj.reshape(dialogs, shard_rows, 3, HEADS, head_dim)
    by_heads = lax.all_to_all(teacher_proj, "seq", split_axis=3, concat_axis=1, tiled=True)
    head_out = jax.vmap(teacher_direct)(by_heads, key_bias)
    heads_here = head_out.shape[2]
    head_out = head_out.reshape(dialogs, seq_count, shard_rows, heads_here, head_dim)
    by_frames = lax.all_to_all(head_out, "seq", split_axis=1, concat_axis=1, tiled=True)
    teacher_vel = jnp.einsum(
        "bsfhd,shdn->bfn",
        by_frames,
        teacher_out.reshape(seq_count, heads_here, head_dim, model_width),
        preferred_element_type=jnp.float32,
    ).reshape(dialogs * shard_rows, model_width)
    offset = seq_index * shard_rows
    queries = jnp.dot(flat_rows, w_inputs[0], preferred_element_type=jnp.float32).astype(
        jnp.bfloat16
    )
    queries = queries.reshape(dialogs, shard_rows, HEADS, head_dim)
    key_local = jnp.dot(flat_rows, w_inputs[1], preferred_element_type=jnp.float32).astype(
        jnp.bfloat16
    )
    value_local = jnp.dot(flat_rows, w_inputs[2], preferred_element_type=jnp.float32).astype(
        jnp.bfloat16
    )
    both_local = jnp.concatenate((key_local, value_local), axis=-1).reshape(
        dialogs, shard_rows, 2 * model_width
    )
    both_window = with_halo(both_local, (("seq", 1),), HALO)
    key_rows = both_window[:, :, :model_width].reshape(dialogs, window, HEADS, head_dim)
    value_rows = both_window[:, :, model_width:].reshape(dialogs, window, HEADS, head_dim)
    group_pad = jnp.pad(group_ids, ((0, 0), (HALO, HALO)), constant_values=-10)
    key_group = lax.dynamic_slice_in_dim(group_pad, offset, window, 1)
    query_group = lax.dynamic_slice_in_dim(group_ids, offset, shard_rows, 1)
    query_pos = offset + jnp.arange(shard_rows, dtype=jnp.int32)
    key_pos = offset - HALO + jnp.arange(window, dtype=jnp.int32)
    allowed = build_allowed(query_group, query_pos, key_group, key_pos, lengths)
    scaling = head_dim ** (-0.5)
    scores = jnp.einsum("brhd,bwhd->bhrw", queries, key_rows, preferred_element_type=jnp.float32)
    scores = jnp.where(allowed[:, None], scores * scaling, NEGATIVE)
    row_max = jnp.max(scores, axis=-1, keepdims=True)
    exponent = jnp.exp(scores - row_max)
    probs = exponent / jnp.sum(exponent, axis=-1, keepdims=True)
    probs_low = probs.astype(jnp.bfloat16)
    student_mix = jnp.einsum(
        "bhrw,bwhd->brhd", probs_low, value_rows, preferred_element_type=jnp.float32
    ).astype(jnp.bfloat16)
    mix_flat = student_mix.reshape(dialogs * shard_rows, model_width)
    student_vel = jnp.dot(mix_flat, w_output, preferred_element_type=jnp.float32)
    query_valid = (query_pos[None, :] < lengths[:, None]).reshape(-1)
    difference = jnp.where(query_valid[:, None], student_vel - teacher_vel, 0.0)
    square_local = jnp.sum(difference * difference)
    count_local = jnp.sum(query_valid.astype(jnp.float32))
    grad_vel = difference.astype(jnp.bfloat16)
    grad_mix = jnp.dot(grad_vel, w_output.T, preferred_element_type=jnp.float32).astype(
        jnp.bfloat16
    )
    grad_mix = grad_mix.reshape(dialogs, shard_rows, HEADS, head_dim)
    grad_prob = jnp.einsum(
        "brhd,bwhd->bhrw", grad_mix, value_rows, preferred_element_type=jnp.float32
    )
    grad_score = probs * (grad_prob - jnp.sum(probs * grad_prob, axis=-1, keepdims=True)) * scaling
    grad_score = lax.optimization_barrier(grad_score)
    grad_key = split_product("bhrw,brhd->bwhd", grad_score, queries, True)
    grad_value = jnp.einsum(
        "bhrw,brhd->bwhd", probs_low, grad_mix, preferred_element_type=jnp.float32
    )
    grad_both = jnp.concatenate(
        (
            grad_key.reshape(dialogs, window, model_width),
            grad_value.reshape(dialogs, window, model_width),
        ),
        axis=-1,
    )
    from_next = from_behind(grad_both[:, :HALO].astype(jnp.bfloat16), "seq", -1).astype(jnp.float32)
    from_prev = from_behind(
        grad_both[:, HALO + shard_rows :].astype(jnp.bfloat16), "seq", 1
    ).astype(jnp.float32)
    owned_rows = grad_both[:, HALO : HALO + shard_rows]
    if shard_rows >= 2 * HALO:
        middle = jnp.zeros((dialogs, shard_rows - 2 * HALO, 2 * model_width), jnp.float32)
        owned_rows = owned_rows + jnp.concatenate((from_prev, middle, from_next), axis=1)
    else:
        owned_rows = owned_rows.at[:, :HALO].add(from_prev)
        owned_rows = owned_rows.at[:, shard_rows - HALO :].add(from_next)
    by_head = owned_rows.reshape(shard_rows, 2, HEADS, head_dim).transpose(0, 2, 1, 3)
    head_grads = lax.all_to_all(
        by_head.astype(jnp.bfloat16), "seq", split_axis=1, concat_axis=0, tiled=True
    )
    head_grads = head_grads.reshape(frames, 2 * head_dim)
    normed_all = lax.all_gather(flat_rows, "seq", axis=0, tiled=True)
    partial = jnp.dot(normed_all.T, head_grads, preferred_element_type=jnp.float32)
    dp_count = lax.axis_size("dp")
    block = rows_each * 2 * head_dim
    partial = partial.reshape(dp_count * seq_count, block)
    lane = jnp.arange(2 * head_dim)
    square_high = lax.reduce_precision(square_local, exponent_bits=8, mantissa_bits=7)
    square_low = square_local - square_high
    scalars = jnp.where(
        lane == 0,
        square_high,
        jnp.where(lane == 1, square_low, jnp.where(lane == 2, count_local, 0.0)),
    )
    partial = jnp.concatenate(
        (partial, jnp.broadcast_to(scalars, (dp_count * seq_count, 2 * head_dim))), axis=1
    ).astype(jnp.bfloat16)
    mine = lax.all_to_all(partial, ("dp", "seq"), split_axis=0, concat_axis=0, tiled=True)
    mine = mine.astype(jnp.float32).reshape(dp_count, seq_count, block + 2 * head_dim)
    totals = mine[:, :, block:].sum((0, 1))
    square_sum, frame_count = totals[0] + totals[1], totals[2]
    mean_error = square_sum / (frame_count * model_width)
    mine = mine[:, :, :block].sum(0) * lax.rsqrt(frame_count)
    mine = mine.reshape(HEADS, rows_each, 2, head_dim).transpose(2, 1, 0, 3)
    grad_inputs = mine.reshape(2, rows_each, model_width)
    return (grad_inputs, mean_error)


def solution(mesh):
    in_specs = (
        P("dp", "seq", None),
        P("dp", "seq", None),
        P("dp"),
        P("dp", None),
        P("dp"),
        P(),
        P(),
        P(),
        P(None, ("dp", "seq"), None),
        P(("dp", "seq"), None),
    )
    out_specs = (P(None, ("dp", "seq"), None), P())
    return jax.shard_map(shards, mesh=mesh, in_specs=in_specs, out_specs=out_specs, check_vma=False)
```

```python
import jax
import jax.numpy as jnp
from jax import lax
from jax.sharding import PartitionSpec as P

HEADS = 16
HALO = 64
TSTEPS = 1000


EPSILON = 1e-06
NEGATIVE = -1e30


def with_halo(block, sides, width):
    for axis, dim in sides:
        count = lax.axis_size(axis)
        forward = [(i, i + 1) for i in range(count - 1)]
        backward = [(target, source) for source, target in forward]
        low = lax.ppermute(
            lax.slice_in_dim(block, block.shape[dim] - width, None, axis=dim), axis, forward
        )
        high = lax.ppermute(lax.slice_in_dim(block, 0, width, axis=dim), axis, backward)
        block = jnp.concatenate([low, block, high], axis=dim)
    return block


def from_behind(block, axis, distance):
    devices = range(lax.axis_size(axis))
    route = [(i - distance, i) for i in devices if i - distance in devices]
    return lax.ppermute(block, axis, route)


def normalize(clean_frames, noise_frames, time_index, modulation):
    flow_time = (time_index.astype(jnp.float32) + 0.5) / TSTEPS
    flow_time = flow_time[:, None, None]
    blended = (1.0 - flow_time) * noise_frames.astype(
        jnp.float32
    ) + flow_time * clean_frames.astype(jnp.float32)
    inv_rms = lax.rsqrt(jnp.mean(blended * blended, axis=-1, keepdims=True) + EPSILON)
    return (blended * inv_rms * (1.0 + flow_time * modulation)).astype(jnp.bfloat16)


def attend_block(queries, key_rows, values, key_bias):
    scores = jnp.dot(queries, key_rows.T, preferred_element_type=jnp.float32) * queries.shape[
        -1
    ] ** (-0.5)
    scores = scores + key_bias[None, :]
    row_max = jnp.max(scores, axis=-1, keepdims=True)
    exponent = jnp.exp(scores - row_max)
    probs_low = (exponent / jnp.sum(exponent, axis=-1, keepdims=True)).astype(jnp.bfloat16)
    return jnp.dot(probs_low, values, preferred_element_type=jnp.float32).astype(jnp.bfloat16)


def full_attention(queries, key_rows, values, key_bias):
    total_rows = queries.shape[0]
    block_rows = min(512, total_rows)
    blocked = queries.reshape(total_rows // block_rows, block_rows, queries.shape[1])
    result = lax.map(lambda piece: attend_block(piece, key_rows, values, key_bias), blocked)
    return result.reshape(total_rows, values.shape[1])


def teacher_heads(proj_one, bias_one):
    stacked = jnp.transpose(proj_one, (2, 1, 0, 3))
    result = lax.map(
        lambda element: full_attention(element[0], element[1], element[2], bias_one), stacked
    )
    return jnp.transpose(result, (1, 0, 2))


def teacher_direct(proj_one, bias_one):
    def one_head(part):
        return attend_block(part[:, 0], part[:, 1], part[:, 2], bias_one)

    return jax.vmap(one_head, in_axes=2, out_axes=1)(proj_one)


def build_allowed(query_group, query_pos, key_group, key_pos, lengths):
    same_group = key_group[:, None, :] == query_group[:, :, None]
    prev_group = key_group[:, None, :] == query_group[:, :, None] - 1
    live_key = (key_pos[None, :] < lengths[:, None]) & (key_pos[None, :] >= 0)
    itself = key_pos[None, :] == query_pos[:, None]
    return (same_group | prev_group) & (live_key[:, None, :] | itself[None])


def split_product(form, gradient, other, first):
    upper_part = gradient.astype(jnp.bfloat16)
    lower_part = (gradient - upper_part.astype(jnp.float32)).astype(jnp.bfloat16)
    if first:
        return jnp.einsum(form, upper_part, other, preferred_element_type=jnp.float32) + jnp.einsum(
            form, lower_part, other, preferred_element_type=jnp.float32
        )
    return jnp.einsum(form, other, upper_part, preferred_element_type=jnp.float32) + jnp.einsum(
        form, other, lower_part, preferred_element_type=jnp.float32
    )


def shards(
    clean_frames,
    noise_frames,
    lengths,
    group_ids,
    time_index,
    modulation,
    teacher_qkv,
    teacher_out,
    student_in,
    student_out,
):
    dialogs, shard_rows, model_width = clean_frames.shape
    head_dim = model_width // HEADS
    seq_count = lax.axis_size("seq")
    seq_index = lax.axis_index("seq")
    frames = shard_rows * seq_count
    window = shard_rows + 2 * HALO
    rows_each = student_out.shape[0]
    stacked = jnp.concatenate((student_in, student_out[None]), axis=0)
    gathered = lax.all_gather(
        lax.all_gather(stacked, "seq", axis=1, tiled=True), "dp", axis=1, tiled=True
    )
    w_inputs = gathered[:3]
    w_output = gathered[3]
    normed = normalize(clean_frames, noise_frames, time_index, modulation)
    flat_rows = normed.reshape(dialogs * shard_rows, model_width)
    frame_pos = jnp.arange(frames, dtype=jnp.int32)
    key_bias = jnp.where(frame_pos[None, :] < lengths[:, None], 0.0, NEGATIVE).astype(jnp.float32)
    teacher_proj = jnp.dot(flat_rows, teacher_qkv, preferred_element_type=jnp.float32).astype(
        jnp.bfloat16
    )
    teacher_proj = teacher_proj.reshape(dialogs, shard_rows, 3, HEADS, head_dim)
    by_heads = lax.all_to_all(teacher_proj, "seq", split_axis=3, concat_axis=1, tiled=True)
    head_out = jax.vmap(teacher_direct)(by_heads, key_bias)
    heads_here = head_out.shape[2]
    head_out = head_out.reshape(dialogs, seq_count, shard_rows, heads_here, head_dim)
    by_frames = lax.all_to_all(head_out, "seq", split_axis=1, concat_axis=1, tiled=True)
    teacher_vel = jnp.einsum(
        "bsfhd,shdn->bfn",
        by_frames,
        teacher_out.reshape(seq_count, heads_here, head_dim, model_width),
        preferred_element_type=jnp.float32,
    ).reshape(dialogs * shard_rows, model_width)
    offset = seq_index * shard_rows
    queries = jnp.dot(flat_rows, w_inputs[0], preferred_element_type=jnp.float32).astype(
        jnp.bfloat16
    )
    queries = queries.reshape(dialogs, shard_rows, HEADS, head_dim)
    key_local = jnp.dot(flat_rows, w_inputs[1], preferred_element_type=jnp.float32).astype(
        jnp.bfloat16
    )
    value_local = jnp.dot(flat_rows, w_inputs[2], preferred_element_type=jnp.float32).astype(
        jnp.bfloat16
    )
    both_local = jnp.concatenate((key_local, value_local), axis=-1).reshape(
        dialogs, shard_rows, 2 * model_width
    )
    both_window = with_halo(both_local, (("seq", 1),), HALO)
    key_rows = both_window[:, :, :model_width].reshape(dialogs, window, HEADS, head_dim)
    value_rows = both_window[:, :, model_width:].reshape(dialogs, window, HEADS, head_dim)
    group_pad = jnp.pad(group_ids, ((0, 0), (HALO, HALO)), constant_values=-10)
    key_group = lax.dynamic_slice_in_dim(group_pad, offset, window, 1)
    query_group = lax.dynamic_slice_in_dim(group_ids, offset, shard_rows, 1)
    query_pos = offset + jnp.arange(shard_rows, dtype=jnp.int32)
    key_pos = offset - HALO + jnp.arange(window, dtype=jnp.int32)
    allowed = build_allowed(query_group, query_pos, key_group, key_pos, lengths)
    scaling = head_dim ** (-0.5)
    scores = jnp.einsum("brhd,bwhd->bhrw", queries, key_rows, preferred_element_type=jnp.float32)
    scores = jnp.where(allowed[:, None], scores * scaling, NEGATIVE)
    row_max = jnp.max(scores, axis=-1, keepdims=True)
    exponent = jnp.exp(scores - row_max)
    probs = exponent / jnp.sum(exponent, axis=-1, keepdims=True)
    probs_low = probs.astype(jnp.bfloat16)
    student_mix = jnp.einsum(
        "bhrw,bwhd->brhd", probs_low, value_rows, preferred_element_type=jnp.float32
    ).astype(jnp.bfloat16)
    mix_flat = student_mix.reshape(dialogs * shard_rows, model_width)
    student_vel = jnp.dot(mix_flat, w_output, preferred_element_type=jnp.float32)
    query_valid = (query_pos[None, :] < lengths[:, None]).reshape(-1)
    difference = jnp.where(query_valid[:, None], student_vel - teacher_vel, 0.0)
    square_local = jnp.sum(difference * difference)
    count_local = jnp.sum(query_valid.astype(jnp.float32))
    grad_vel = difference.astype(jnp.bfloat16)
    grad_mix = jnp.dot(grad_vel, w_output.T, preferred_element_type=jnp.float32).astype(
        jnp.bfloat16
    )
    grad_mix = grad_mix.reshape(dialogs, shard_rows, HEADS, head_dim)
    grad_prob = jnp.einsum(
        "brhd,bwhd->bhrw", grad_mix, value_rows, preferred_element_type=jnp.float32
    )
    grad_score = probs * (grad_prob - jnp.sum(probs * grad_prob, axis=-1, keepdims=True)) * scaling
    grad_score = lax.optimization_barrier(grad_score)
    grad_key = split_product("bhrw,brhd->bwhd", grad_score, queries, True)
    grad_value = jnp.einsum(
        "bhrw,brhd->bwhd", probs_low, grad_mix, preferred_element_type=jnp.float32
    )
    grad_both = jnp.concatenate(
        (
            grad_key.reshape(dialogs, window, model_width),
            grad_value.reshape(dialogs, window, model_width),
        ),
        axis=-1,
    )
    by_head = grad_both.reshape(window, 2, HEADS, head_dim).transpose(0, 2, 1, 3)
    windows = lax.all_to_all(
        by_head.astype(jnp.bfloat16), "seq", split_axis=1, concat_axis=0, tiled=True
    )
    windows = windows.reshape(seq_count, window, 2 * head_dim).astype(jnp.float32)
    blank = jnp.zeros((1, HALO, 2 * head_dim), jnp.float32)
    from_prev = jnp.concatenate((blank, windows[:-1, HALO + shard_rows :]), axis=0)
    from_next = jnp.concatenate((windows[1:, :HALO], blank), axis=0)
    owned_rows = windows[:, HALO : HALO + shard_rows]
    if shard_rows >= 2 * HALO:
        middle = jnp.zeros((seq_count, shard_rows - 2 * HALO, 2 * head_dim), jnp.float32)
        owned_rows = owned_rows + jnp.concatenate((from_prev, middle, from_next), axis=1)
    else:
        owned_rows = owned_rows.at[:, :HALO].add(from_prev)
        owned_rows = owned_rows.at[:, shard_rows - HALO :].add(from_next)
    head_grads = owned_rows.reshape(frames, 2 * head_dim).astype(jnp.bfloat16)
    normed_all = lax.all_gather(flat_rows, "seq", axis=0, tiled=True)
    partial = jnp.dot(normed_all.T, head_grads, preferred_element_type=jnp.float32)
    dp_count = lax.axis_size("dp")
    block = rows_each * 2 * head_dim
    partial = partial.reshape(dp_count * seq_count, block)
    lane = jnp.arange(2 * head_dim)
    scalars = jnp.where(lane == 0, square_local, jnp.where(lane == 1, count_local, 0.0))
    partial = jnp.concatenate(
        (partial, jnp.broadcast_to(scalars, (dp_count * seq_count, 2 * head_dim))), axis=1
    )
    mine = lax.all_to_all(partial, ("dp", "seq"), split_axis=0, concat_axis=0, tiled=True)
    mine = mine.reshape(dp_count, seq_count, block + 2 * head_dim)
    totals = mine[:, :, block:].sum((0, 1))
    square_sum, frame_count = totals[0], totals[1]
    mean_error = square_sum / (frame_count * model_width)
    mine = mine[:, :, :block].sum(0) * lax.rsqrt(frame_count)
    mine = mine.reshape(HEADS, rows_each, 2, head_dim).transpose(2, 1, 0, 3)
    grad_inputs = mine.reshape(2, rows_each, model_width)
    return (grad_inputs, mean_error)


def solution(mesh):
    in_specs = (
        P("dp", "seq", None),
        P("dp", "seq", None),
        P("dp"),
        P("dp", None),
        P("dp"),
        P(),
        P(),
        P(),
        P(None, ("dp", "seq"), None),
        P(("dp", "seq"), None),
    )
    out_specs = (P(None, ("dp", "seq"), None), P())
    return jax.shard_map(shards, mesh=mesh, in_specs=in_specs, out_specs=out_specs, check_vma=False)
```

```python
import jax
import jax.numpy as jnp
from jax import lax
from jax.sharding import PartitionSpec as P

HEADS = 16
HALO = 64
TSTEPS = 1000


EPSILON = 1e-06
NEGATIVE = -1e30


def with_halo(block, sides, width):
    for axis, dim in sides:
        count = lax.axis_size(axis)
        forward = [(i, i + 1) for i in range(count - 1)]
        backward = [(target, source) for source, target in forward]
        low = lax.ppermute(
            lax.slice_in_dim(block, block.shape[dim] - width, None, axis=dim), axis, forward
        )
        high = lax.ppermute(lax.slice_in_dim(block, 0, width, axis=dim), axis, backward)
        block = jnp.concatenate([low, block, high], axis=dim)
    return block


def from_behind(block, axis, distance):
    devices = range(lax.axis_size(axis))
    route = [(i - distance, i) for i in devices if i - distance in devices]
    return lax.ppermute(block, axis, route)


def normalize(clean_frames, noise_frames, time_index, modulation):
    flow_time = (time_index.astype(jnp.float32) + 0.5) / TSTEPS
    flow_time = flow_time[:, None, None]
    blended = (1.0 - flow_time) * noise_frames.astype(
        jnp.float32
    ) + flow_time * clean_frames.astype(jnp.float32)
    inv_rms = lax.rsqrt(jnp.mean(blended * blended, axis=-1, keepdims=True) + EPSILON)
    return (blended * inv_rms * (1.0 + flow_time * modulation)).astype(jnp.bfloat16)


def attend_block(queries, key_rows, values, key_bias):
    scores = jnp.dot(queries, key_rows.T, preferred_element_type=jnp.float32) * queries.shape[
        -1
    ] ** (-0.5)
    scores = scores + key_bias[None, :]
    row_max = jnp.max(scores, axis=-1, keepdims=True)
    exponent = jnp.exp(scores - row_max)
    probs_low = (exponent / jnp.sum(exponent, axis=-1, keepdims=True)).astype(jnp.bfloat16)
    return jnp.dot(probs_low, values, preferred_element_type=jnp.float32).astype(jnp.bfloat16)


def full_attention(queries, key_rows, values, key_bias):
    total_rows = queries.shape[0]
    block_rows = min(512, total_rows)
    blocked = queries.reshape(total_rows // block_rows, block_rows, queries.shape[1])
    result = lax.map(lambda piece: attend_block(piece, key_rows, values, key_bias), blocked)
    return result.reshape(total_rows, values.shape[1])


def teacher_heads(proj_one, bias_one):
    stacked = jnp.transpose(proj_one, (2, 1, 0, 3))
    result = lax.map(
        lambda element: full_attention(element[0], element[1], element[2], bias_one), stacked
    )
    return jnp.transpose(result, (1, 0, 2))


def teacher_direct(proj_one, bias_one):
    def one_head(part):
        return attend_block(part[:, 0], part[:, 1], part[:, 2], bias_one)

    return jax.vmap(one_head, in_axes=2, out_axes=1)(proj_one)


def build_allowed(query_group, query_pos, key_group, key_pos, lengths):
    same_group = key_group[:, None, :] == query_group[:, :, None]
    prev_group = key_group[:, None, :] == query_group[:, :, None] - 1
    live_key = (key_pos[None, :] < lengths[:, None]) & (key_pos[None, :] >= 0)
    itself = key_pos[None, :] == query_pos[:, None]
    return (same_group | prev_group) & (live_key[:, None, :] | itself[None])


def split_product(form, gradient, other, first):
    upper_part = gradient.astype(jnp.bfloat16)
    lower_part = (gradient - upper_part.astype(jnp.float32)).astype(jnp.bfloat16)
    if first:
        return jnp.einsum(form, upper_part, other, preferred_element_type=jnp.float32) + jnp.einsum(
            form, lower_part, other, preferred_element_type=jnp.float32
        )
    return jnp.einsum(form, other, upper_part, preferred_element_type=jnp.float32) + jnp.einsum(
        form, other, lower_part, preferred_element_type=jnp.float32
    )


def shards(
    clean_frames,
    noise_frames,
    lengths,
    group_ids,
    time_index,
    modulation,
    teacher_qkv,
    teacher_out,
    student_in,
    student_out,
):
    dialogs, shard_rows, model_width = clean_frames.shape
    head_dim = model_width // HEADS
    seq_count = lax.axis_size("seq")
    seq_index = lax.axis_index("seq")
    frames = shard_rows * seq_count
    window = shard_rows + 2 * HALO
    rows_each = student_out.shape[0]
    stacked = jnp.concatenate((student_in, student_out[None]), axis=0)
    gathered = lax.all_gather(
        lax.all_gather(stacked, "seq", axis=1, tiled=True), "dp", axis=1, tiled=True
    )
    w_inputs = gathered[:3]
    w_output = gathered[3]
    normed = normalize(clean_frames, noise_frames, time_index, modulation)
    flat_rows = normed.reshape(dialogs * shard_rows, model_width)
    frame_pos = jnp.arange(frames, dtype=jnp.int32)
    key_bias = jnp.where(frame_pos[None, :] < lengths[:, None], 0.0, NEGATIVE).astype(jnp.float32)
    teacher_proj = jnp.dot(flat_rows, teacher_qkv, preferred_element_type=jnp.float32).astype(
        jnp.bfloat16
    )
    teacher_proj = teacher_proj.reshape(dialogs, shard_rows, 3, HEADS, head_dim)
    by_heads = lax.all_to_all(teacher_proj, "seq", split_axis=3, concat_axis=1, tiled=True)
    head_out = jax.vmap(teacher_direct)(by_heads, key_bias)
    normed_all = lax.all_to_all(
        jnp.broadcast_to(flat_rows[None], (seq_count,) + flat_rows.shape),
        "seq",
        split_axis=0,
        concat_axis=0,
        tiled=True,
    ).reshape(-1, model_width)
    normed_all, head_out = lax.optimization_barrier((normed_all, head_out))
    heads_here = head_out.shape[2]
    head_out = head_out.reshape(dialogs, seq_count, shard_rows, heads_here, head_dim)
    by_frames = lax.all_to_all(head_out, "seq", split_axis=1, concat_axis=1, tiled=True)
    teacher_vel = jnp.einsum(
        "bsfhd,shdn->bfn",
        by_frames,
        teacher_out.reshape(seq_count, heads_here, head_dim, model_width),
        preferred_element_type=jnp.float32,
    ).reshape(dialogs * shard_rows, model_width)
    offset = seq_index * shard_rows
    queries = jnp.dot(flat_rows, w_inputs[0], preferred_element_type=jnp.float32).astype(
        jnp.bfloat16
    )
    queries = queries.reshape(dialogs, shard_rows, HEADS, head_dim)
    key_local = jnp.dot(flat_rows, w_inputs[1], preferred_element_type=jnp.float32).astype(
        jnp.bfloat16
    )
    value_local = jnp.dot(flat_rows, w_inputs[2], preferred_element_type=jnp.float32).astype(
        jnp.bfloat16
    )
    both_local = jnp.concatenate((key_local, value_local), axis=-1).reshape(
        dialogs, shard_rows, 2 * model_width
    )
    both_window = with_halo(both_local, (("seq", 1),), HALO)
    key_rows = both_window[:, :, :model_width].reshape(dialogs, window, HEADS, head_dim)
    value_rows = both_window[:, :, model_width:].reshape(dialogs, window, HEADS, head_dim)
    group_pad = jnp.pad(group_ids, ((0, 0), (HALO, HALO)), constant_values=-10)
    key_group = lax.dynamic_slice_in_dim(group_pad, offset, window, 1)
    query_group = lax.dynamic_slice_in_dim(group_ids, offset, shard_rows, 1)
    query_pos = offset + jnp.arange(shard_rows, dtype=jnp.int32)
    key_pos = offset - HALO + jnp.arange(window, dtype=jnp.int32)
    allowed = build_allowed(query_group, query_pos, key_group, key_pos, lengths)
    scaling = head_dim ** (-0.5)
    scores = jnp.einsum("brhd,bwhd->bhrw", queries, key_rows, preferred_element_type=jnp.float32)
    scores = jnp.where(allowed[:, None], scores * scaling, NEGATIVE)
    row_max = jnp.max(scores, axis=-1, keepdims=True)
    exponent = jnp.exp(scores - row_max)
    probs = exponent / jnp.sum(exponent, axis=-1, keepdims=True)
    probs_low = probs.astype(jnp.bfloat16)
    student_mix = jnp.einsum(
        "bhrw,bwhd->brhd", probs_low, value_rows, preferred_element_type=jnp.float32
    ).astype(jnp.bfloat16)
    mix_flat = student_mix.reshape(dialogs * shard_rows, model_width)
    student_vel = jnp.dot(mix_flat, w_output, preferred_element_type=jnp.float32)
    query_valid = (query_pos[None, :] < lengths[:, None]).reshape(-1)
    difference = jnp.where(query_valid[:, None], student_vel - teacher_vel, 0.0)
    square_local = jnp.sum(difference * difference)
    count_local = jnp.sum(query_valid.astype(jnp.float32))
    grad_vel = difference.astype(jnp.bfloat16)
    grad_mix = jnp.dot(grad_vel, w_output.T, preferred_element_type=jnp.float32).astype(
        jnp.bfloat16
    )
    grad_mix = grad_mix.reshape(dialogs, shard_rows, HEADS, head_dim)
    grad_prob = jnp.einsum(
        "brhd,bwhd->bhrw", grad_mix, value_rows, preferred_element_type=jnp.float32
    )
    grad_score = probs * (grad_prob - jnp.sum(probs * grad_prob, axis=-1, keepdims=True)) * scaling
    grad_score = lax.optimization_barrier(grad_score)
    grad_key = split_product("bhrw,brhd->bwhd", grad_score, queries, True)
    grad_value = jnp.einsum(
        "bhrw,brhd->bwhd", probs_low, grad_mix, preferred_element_type=jnp.float32
    )
    grad_both = jnp.concatenate(
        (
            grad_key.reshape(dialogs, window, model_width),
            grad_value.reshape(dialogs, window, model_width),
        ),
        axis=-1,
    )
    by_head = grad_both.reshape(window, 2, HEADS, head_dim).transpose(0, 2, 1, 3)
    windows = lax.all_to_all(
        by_head.astype(jnp.bfloat16), "seq", split_axis=1, concat_axis=0, tiled=True
    )
    windows = windows.reshape(seq_count, window, 2 * head_dim).astype(jnp.float32)
    blank = jnp.zeros((1, HALO, 2 * head_dim), jnp.float32)
    from_prev = jnp.concatenate((blank, windows[:-1, HALO + shard_rows :]), axis=0)
    from_next = jnp.concatenate((windows[1:, :HALO], blank), axis=0)
    owned_rows = windows[:, HALO : HALO + shard_rows]
    if shard_rows >= 2 * HALO:
        middle = jnp.zeros((seq_count, shard_rows - 2 * HALO, 2 * head_dim), jnp.float32)
        owned_rows = owned_rows + jnp.concatenate((from_prev, middle, from_next), axis=1)
    else:
        owned_rows = owned_rows.at[:, :HALO].add(from_prev)
        owned_rows = owned_rows.at[:, shard_rows - HALO :].add(from_next)
    head_grads = owned_rows.reshape(frames, 2 * head_dim).astype(jnp.bfloat16)
    partial = jnp.dot(normed_all.T, head_grads, preferred_element_type=jnp.float32)
    dp_count = lax.axis_size("dp")
    block = rows_each * 2 * head_dim
    partial = partial.reshape(dp_count * seq_count, block)
    lane = jnp.arange(2 * head_dim)
    scalars = jnp.where(lane == 0, square_local, jnp.where(lane == 1, count_local, 0.0))
    partial = jnp.concatenate(
        (partial, jnp.broadcast_to(scalars, (dp_count * seq_count, 2 * head_dim))), axis=1
    )
    mine = lax.all_to_all(partial, ("dp", "seq"), split_axis=0, concat_axis=0, tiled=True)
    mine = mine.reshape(dp_count, seq_count, block + 2 * head_dim)
    totals = mine[:, :, block:].sum((0, 1))
    square_sum, frame_count = totals[0], totals[1]
    mean_error = square_sum / (frame_count * model_width)
    mine = mine[:, :, :block].sum(0) * lax.rsqrt(frame_count)
    mine = mine.reshape(HEADS, rows_each, 2, head_dim).transpose(2, 1, 0, 3)
    grad_inputs = mine.reshape(2, rows_each, model_width)
    return (grad_inputs, mean_error)


def solution(mesh):
    in_specs = (
        P("dp", "seq", None),
        P("dp", "seq", None),
        P("dp"),
        P("dp", None),
        P("dp"),
        P(),
        P(),
        P(),
        P(None, ("dp", "seq"), None),
        P(("dp", "seq"), None),
    )
    out_specs = (P(None, ("dp", "seq"), None), P())
    return jax.shard_map(shards, mesh=mesh, in_specs=in_specs, out_specs=out_specs, check_vma=False)
```

```python
import jax
import jax.numpy as jnp
from jax import lax
from jax.sharding import PartitionSpec as P

HEADS = 16
HALO = 64
TSTEPS = 1000


EPSILON = 1e-06
NEGATIVE = -1e30


def with_halo(block, sides, width):
    for axis, dim in sides:
        count = lax.axis_size(axis)
        forward = [(i, i + 1) for i in range(count - 1)]
        backward = [(target, source) for source, target in forward]
        low = lax.ppermute(
            lax.slice_in_dim(block, block.shape[dim] - width, None, axis=dim), axis, forward
        )
        high = lax.ppermute(lax.slice_in_dim(block, 0, width, axis=dim), axis, backward)
        block = jnp.concatenate([low, block, high], axis=dim)
    return block


def doubling_gather(block, axis, dim):
    count = lax.axis_size(axis)
    index = lax.axis_index(axis)
    step = 1
    while step < count:
        pairs = [(i, i ^ step) for i in range(count)]
        other = lax.ppermute(block, axis, pairs)
        upper = (index & step) != 0
        block = jnp.where(
            upper,
            jnp.concatenate((other, block), axis=dim),
            jnp.concatenate((block, other), axis=dim),
        )
        step *= 2
    return block


def from_behind(block, axis, distance):
    devices = range(lax.axis_size(axis))
    route = [(i - distance, i) for i in devices if i - distance in devices]
    return lax.ppermute(block, axis, route)


def normalize(clean_frames, noise_frames, time_index, modulation):
    flow_time = (time_index.astype(jnp.float32) + 0.5) / TSTEPS
    flow_time = flow_time[:, None, None]
    blended = (1.0 - flow_time) * noise_frames.astype(
        jnp.float32
    ) + flow_time * clean_frames.astype(jnp.float32)
    inv_rms = lax.rsqrt(jnp.mean(blended * blended, axis=-1, keepdims=True) + EPSILON)
    return (blended * inv_rms * (1.0 + flow_time * modulation)).astype(jnp.bfloat16)


def attend_block(queries, key_rows, values, key_bias):
    scores = jnp.dot(queries, key_rows.T, preferred_element_type=jnp.float32) * queries.shape[
        -1
    ] ** (-0.5)
    scores = scores + key_bias[None, :]
    row_max = jnp.max(scores, axis=-1, keepdims=True)
    exponent = jnp.exp(scores - row_max)
    probs_low = (exponent / jnp.sum(exponent, axis=-1, keepdims=True)).astype(jnp.bfloat16)
    return jnp.dot(probs_low, values, preferred_element_type=jnp.float32).astype(jnp.bfloat16)


def full_attention(queries, key_rows, values, key_bias):
    total_rows = queries.shape[0]
    block_rows = min(512, total_rows)
    blocked = queries.reshape(total_rows // block_rows, block_rows, queries.shape[1])
    result = lax.map(lambda piece: attend_block(piece, key_rows, values, key_bias), blocked)
    return result.reshape(total_rows, values.shape[1])


def teacher_heads(proj_one, bias_one):
    stacked = jnp.transpose(proj_one, (2, 1, 0, 3))
    result = lax.map(
        lambda element: full_attention(element[0], element[1], element[2], bias_one), stacked
    )
    return jnp.transpose(result, (1, 0, 2))


def teacher_direct(proj_one, bias_one):
    def one_head(part):
        return attend_block(part[:, 0], part[:, 1], part[:, 2], bias_one)

    return jax.vmap(one_head, in_axes=2, out_axes=1)(proj_one)


def build_allowed(query_group, query_pos, key_group, key_pos, lengths):
    same_group = key_group[:, None, :] == query_group[:, :, None]
    prev_group = key_group[:, None, :] == query_group[:, :, None] - 1
    live_key = (key_pos[None, :] < lengths[:, None]) & (key_pos[None, :] >= 0)
    itself = key_pos[None, :] == query_pos[:, None]
    return (same_group | prev_group) & (live_key[:, None, :] | itself[None])


def split_product(form, gradient, other, first):
    upper_part = gradient.astype(jnp.bfloat16)
    lower_part = (gradient - upper_part.astype(jnp.float32)).astype(jnp.bfloat16)
    if first:
        return jnp.einsum(form, upper_part, other, preferred_element_type=jnp.float32) + jnp.einsum(
            form, lower_part, other, preferred_element_type=jnp.float32
        )
    return jnp.einsum(form, other, upper_part, preferred_element_type=jnp.float32) + jnp.einsum(
        form, other, lower_part, preferred_element_type=jnp.float32
    )


def shards(
    clean_frames,
    noise_frames,
    lengths,
    group_ids,
    time_index,
    modulation,
    teacher_qkv,
    teacher_out,
    student_in,
    student_out,
):
    dialogs, shard_rows, model_width = clean_frames.shape
    head_dim = model_width // HEADS
    seq_count = lax.axis_size("seq")
    seq_index = lax.axis_index("seq")
    frames = shard_rows * seq_count
    window = shard_rows + 2 * HALO
    rows_each = student_out.shape[0]
    stacked = jnp.concatenate((student_in, student_out[None]), axis=0)
    gathered = lax.all_gather(doubling_gather(stacked, "seq", 1), "dp", axis=1, tiled=True)
    w_inputs = gathered[:3]
    w_output = gathered[3]
    normed = normalize(clean_frames, noise_frames, time_index, modulation)
    flat_rows = normed.reshape(dialogs * shard_rows, model_width)
    frame_pos = jnp.arange(frames, dtype=jnp.int32)
    key_bias = jnp.where(frame_pos[None, :] < lengths[:, None], 0.0, NEGATIVE).astype(jnp.float32)
    teacher_proj = jnp.dot(flat_rows, teacher_qkv, preferred_element_type=jnp.float32).astype(
        jnp.bfloat16
    )
    teacher_proj = teacher_proj.reshape(dialogs, shard_rows, 3, HEADS, head_dim)
    by_heads = lax.all_to_all(teacher_proj, "seq", split_axis=3, concat_axis=1, tiled=True)
    head_out = jax.vmap(teacher_direct)(by_heads, key_bias)
    heads_here = head_out.shape[2]
    head_out = head_out.reshape(dialogs, seq_count, shard_rows, heads_here, head_dim)
    by_frames = lax.all_to_all(head_out, "seq", split_axis=1, concat_axis=1, tiled=True)
    teacher_vel = jnp.einsum(
        "bsfhd,shdn->bfn",
        by_frames,
        teacher_out.reshape(seq_count, heads_here, head_dim, model_width),
        preferred_element_type=jnp.float32,
    ).reshape(dialogs * shard_rows, model_width)
    offset = seq_index * shard_rows
    queries = jnp.dot(flat_rows, w_inputs[0], preferred_element_type=jnp.float32).astype(
        jnp.bfloat16
    )
    queries = queries.reshape(dialogs, shard_rows, HEADS, head_dim)
    key_local = jnp.dot(flat_rows, w_inputs[1], preferred_element_type=jnp.float32).astype(
        jnp.bfloat16
    )
    value_local = jnp.dot(flat_rows, w_inputs[2], preferred_element_type=jnp.float32).astype(
        jnp.bfloat16
    )
    both_local = jnp.concatenate((key_local, value_local), axis=-1).reshape(
        dialogs, shard_rows, 2 * model_width
    )
    both_window = with_halo(both_local, (("seq", 1),), HALO)
    key_rows = both_window[:, :, :model_width].reshape(dialogs, window, HEADS, head_dim)
    value_rows = both_window[:, :, model_width:].reshape(dialogs, window, HEADS, head_dim)
    group_pad = jnp.pad(group_ids, ((0, 0), (HALO, HALO)), constant_values=-10)
    key_group = lax.dynamic_slice_in_dim(group_pad, offset, window, 1)
    query_group = lax.dynamic_slice_in_dim(group_ids, offset, shard_rows, 1)
    query_pos = offset + jnp.arange(shard_rows, dtype=jnp.int32)
    key_pos = offset - HALO + jnp.arange(window, dtype=jnp.int32)
    allowed = build_allowed(query_group, query_pos, key_group, key_pos, lengths)
    scaling = head_dim ** (-0.5)
    scores = jnp.einsum("brhd,bwhd->bhrw", queries, key_rows, preferred_element_type=jnp.float32)
    scores = jnp.where(allowed[:, None], scores * scaling, NEGATIVE)
    row_max = jnp.max(scores, axis=-1, keepdims=True)
    exponent = jnp.exp(scores - row_max)
    probs = exponent / jnp.sum(exponent, axis=-1, keepdims=True)
    probs_low = probs.astype(jnp.bfloat16)
    student_mix = jnp.einsum(
        "bhrw,bwhd->brhd", probs_low, value_rows, preferred_element_type=jnp.float32
    ).astype(jnp.bfloat16)
    mix_flat = student_mix.reshape(dialogs * shard_rows, model_width)
    student_vel = jnp.dot(mix_flat, w_output, preferred_element_type=jnp.float32)
    query_valid = (query_pos[None, :] < lengths[:, None]).reshape(-1)
    difference = jnp.where(query_valid[:, None], student_vel - teacher_vel, 0.0)
    square_local = jnp.sum(difference * difference)
    count_local = jnp.sum(query_valid.astype(jnp.float32))
    grad_vel = difference.astype(jnp.bfloat16)
    grad_mix = jnp.dot(grad_vel, w_output.T, preferred_element_type=jnp.float32).astype(
        jnp.bfloat16
    )
    grad_mix = grad_mix.reshape(dialogs, shard_rows, HEADS, head_dim)
    grad_prob = jnp.einsum(
        "brhd,bwhd->bhrw", grad_mix, value_rows, preferred_element_type=jnp.float32
    )
    grad_score = probs * (grad_prob - jnp.sum(probs * grad_prob, axis=-1, keepdims=True)) * scaling
    grad_score = lax.optimization_barrier(grad_score)
    grad_key = split_product("bhrw,brhd->bwhd", grad_score, queries, True)
    grad_value = jnp.einsum(
        "bhrw,brhd->bwhd", probs_low, grad_mix, preferred_element_type=jnp.float32
    )
    grad_both = jnp.concatenate(
        (
            grad_key.reshape(dialogs, window, model_width),
            grad_value.reshape(dialogs, window, model_width),
        ),
        axis=-1,
    )
    by_head = grad_both.reshape(window, 2, HEADS, head_dim).transpose(0, 2, 1, 3)
    windows = lax.all_to_all(
        by_head.astype(jnp.bfloat16), "seq", split_axis=1, concat_axis=0, tiled=True
    )
    windows = windows.reshape(seq_count, window, 2 * head_dim).astype(jnp.float32)
    blank = jnp.zeros((1, HALO, 2 * head_dim), jnp.float32)
    from_prev = jnp.concatenate((blank, windows[:-1, HALO + shard_rows :]), axis=0)
    from_next = jnp.concatenate((windows[1:, :HALO], blank), axis=0)
    owned_rows = windows[:, HALO : HALO + shard_rows]
    if shard_rows >= 2 * HALO:
        middle = jnp.zeros((seq_count, shard_rows - 2 * HALO, 2 * head_dim), jnp.float32)
        owned_rows = owned_rows + jnp.concatenate((from_prev, middle, from_next), axis=1)
    else:
        owned_rows = owned_rows.at[:, :HALO].add(from_prev)
        owned_rows = owned_rows.at[:, shard_rows - HALO :].add(from_next)
    head_grads = owned_rows.reshape(frames, 2 * head_dim).astype(jnp.bfloat16)
    normed_all = lax.all_gather(flat_rows, "seq", axis=0, tiled=True)
    partial = jnp.dot(normed_all.T, head_grads, preferred_element_type=jnp.float32)
    dp_count = lax.axis_size("dp")
    block = rows_each * 2 * head_dim
    partial = partial.reshape(dp_count * seq_count, block)
    lane = jnp.arange(2 * head_dim)
    scalars = jnp.where(lane == 0, square_local, jnp.where(lane == 1, count_local, 0.0))
    partial = jnp.concatenate(
        (partial, jnp.broadcast_to(scalars, (dp_count * seq_count, 2 * head_dim))), axis=1
    )
    mine = lax.all_to_all(partial, ("dp", "seq"), split_axis=0, concat_axis=0, tiled=True)
    mine = mine.reshape(dp_count, seq_count, block + 2 * head_dim)
    totals = mine[:, :, block:].sum((0, 1))
    square_sum, frame_count = totals[0], totals[1]
    mean_error = square_sum / (frame_count * model_width)
    mine = mine[:, :, :block].sum(0) * lax.rsqrt(frame_count)
    mine = mine.reshape(HEADS, rows_each, 2, head_dim).transpose(2, 1, 0, 3)
    grad_inputs = mine.reshape(2, rows_each, model_width)
    return (grad_inputs, mean_error)


def solution(mesh):
    in_specs = (
        P("dp", "seq", None),
        P("dp", "seq", None),
        P("dp"),
        P("dp", None),
        P("dp"),
        P(),
        P(),
        P(),
        P(None, ("dp", "seq"), None),
        P(("dp", "seq"), None),
    )
    out_specs = (P(None, ("dp", "seq"), None), P())
    return jax.shard_map(shards, mesh=mesh, in_specs=in_specs, out_specs=out_specs, check_vma=False)
```

```python
import jax
import jax.numpy as jnp
from jax import lax
from jax.sharding import PartitionSpec as P

HEADS = 16
HALO = 64
TSTEPS = 1000


EPSILON = 1e-06
NEGATIVE = -1e30


def with_halo(block, sides, width):
    for axis, dim in sides:
        count = lax.axis_size(axis)
        forward = [(i, i + 1) for i in range(count - 1)]
        backward = [(target, source) for source, target in forward]
        low = lax.ppermute(
            lax.slice_in_dim(block, block.shape[dim] - width, None, axis=dim), axis, forward
        )
        high = lax.ppermute(lax.slice_in_dim(block, 0, width, axis=dim), axis, backward)
        block = jnp.concatenate([low, block, high], axis=dim)
    return block


def doubling_gather(block, axis, dim):
    count = lax.axis_size(axis)
    index = lax.axis_index(axis)
    step = 1
    while step < count:
        pairs = [(i, i ^ step) for i in range(count)]
        other = lax.ppermute(block, axis, pairs)
        upper = (index & step) != 0
        block = jnp.where(
            upper,
            jnp.concatenate((other, block), axis=dim),
            jnp.concatenate((block, other), axis=dim),
        )
        step *= 2
    return block


def from_behind(block, axis, distance):
    devices = range(lax.axis_size(axis))
    route = [(i - distance, i) for i in devices if i - distance in devices]
    return lax.ppermute(block, axis, route)


def normalize(clean_frames, noise_frames, time_index, modulation):
    flow_time = (time_index.astype(jnp.float32) + 0.5) / TSTEPS
    flow_time = flow_time[:, None, None]
    blended = (1.0 - flow_time) * noise_frames.astype(
        jnp.float32
    ) + flow_time * clean_frames.astype(jnp.float32)
    inv_rms = lax.rsqrt(jnp.mean(blended * blended, axis=-1, keepdims=True) + EPSILON)
    return (blended * inv_rms * (1.0 + flow_time * modulation)).astype(jnp.bfloat16)


def attend_block(queries, key_rows, values, key_bias):
    scores = jnp.dot(queries, key_rows.T, preferred_element_type=jnp.float32) * queries.shape[
        -1
    ] ** (-0.5)
    scores = scores + key_bias[None, :]
    row_max = jnp.max(scores, axis=-1, keepdims=True)
    exponent = jnp.exp(scores - row_max)
    probs_low = (exponent / jnp.sum(exponent, axis=-1, keepdims=True)).astype(jnp.bfloat16)
    return jnp.dot(probs_low, values, preferred_element_type=jnp.float32).astype(jnp.bfloat16)


def full_attention(queries, key_rows, values, key_bias):
    total_rows = queries.shape[0]
    block_rows = min(512, total_rows)
    blocked = queries.reshape(total_rows // block_rows, block_rows, queries.shape[1])
    result = lax.map(lambda piece: attend_block(piece, key_rows, values, key_bias), blocked)
    return result.reshape(total_rows, values.shape[1])


def teacher_heads(proj_one, bias_one):
    stacked = jnp.transpose(proj_one, (2, 1, 0, 3))
    result = lax.map(
        lambda element: full_attention(element[0], element[1], element[2], bias_one), stacked
    )
    return jnp.transpose(result, (1, 0, 2))


def teacher_direct(proj_one, bias_one):
    def one_head(part):
        return attend_block(part[:, 0], part[:, 1], part[:, 2], bias_one)

    return jax.vmap(one_head, in_axes=2, out_axes=1)(proj_one)


def build_allowed(query_group, query_pos, key_group, key_pos, lengths):
    same_group = key_group[:, None, :] == query_group[:, :, None]
    prev_group = key_group[:, None, :] == query_group[:, :, None] - 1
    live_key = (key_pos[None, :] < lengths[:, None]) & (key_pos[None, :] >= 0)
    itself = key_pos[None, :] == query_pos[:, None]
    return (same_group | prev_group) & (live_key[:, None, :] | itself[None])


def split_product(form, gradient, other, first):
    upper_part = gradient.astype(jnp.bfloat16)
    lower_part = (gradient - upper_part.astype(jnp.float32)).astype(jnp.bfloat16)
    if first:
        return jnp.einsum(form, upper_part, other, preferred_element_type=jnp.float32) + jnp.einsum(
            form, lower_part, other, preferred_element_type=jnp.float32
        )
    return jnp.einsum(form, other, upper_part, preferred_element_type=jnp.float32) + jnp.einsum(
        form, other, lower_part, preferred_element_type=jnp.float32
    )


def shards(
    clean_frames,
    noise_frames,
    lengths,
    group_ids,
    time_index,
    modulation,
    teacher_qkv,
    teacher_out,
    student_in,
    student_out,
):
    dialogs, shard_rows, model_width = clean_frames.shape
    head_dim = model_width // HEADS
    seq_count = lax.axis_size("seq")
    seq_index = lax.axis_index("seq")
    frames = shard_rows * seq_count
    window = shard_rows + 2 * HALO
    rows_each = student_out.shape[0]
    stacked = jnp.concatenate((student_in, student_out[None]), axis=0)
    gathered = lax.all_gather(
        lax.all_gather(stacked, "seq", axis=1, tiled=True), "dp", axis=1, tiled=True
    )
    w_inputs = gathered[:3]
    w_output = gathered[3]
    normed = normalize(clean_frames, noise_frames, time_index, modulation)
    flat_rows = normed.reshape(dialogs * shard_rows, model_width)
    frame_pos = jnp.arange(frames, dtype=jnp.int32)
    key_bias = jnp.where(frame_pos[None, :] < lengths[:, None], 0.0, NEGATIVE).astype(jnp.float32)
    teacher_proj = jnp.dot(flat_rows, teacher_qkv, preferred_element_type=jnp.float32).astype(
        jnp.bfloat16
    )
    teacher_proj = teacher_proj.reshape(dialogs, shard_rows, 3, HEADS, head_dim)
    by_heads = lax.all_to_all(teacher_proj, "seq", split_axis=3, concat_axis=1, tiled=True)
    head_out = jax.vmap(teacher_direct)(by_heads, key_bias)
    heads_here = head_out.shape[2]
    head_out = head_out.reshape(dialogs, seq_count, shard_rows, heads_here, head_dim)
    by_frames = lax.all_to_all(head_out, "seq", split_axis=1, concat_axis=1, tiled=True)
    teacher_vel = jnp.einsum(
        "bsfhd,shdn->bfn",
        by_frames,
        teacher_out.reshape(seq_count, heads_here, head_dim, model_width),
        preferred_element_type=jnp.float32,
    ).reshape(dialogs * shard_rows, model_width)
    offset = seq_index * shard_rows
    queries = jnp.dot(flat_rows, w_inputs[0], preferred_element_type=jnp.float32).astype(
        jnp.bfloat16
    )
    queries = queries.reshape(dialogs, shard_rows, HEADS, head_dim)
    key_local = jnp.dot(flat_rows, w_inputs[1], preferred_element_type=jnp.float32).astype(
        jnp.bfloat16
    )
    value_local = jnp.dot(flat_rows, w_inputs[2], preferred_element_type=jnp.float32).astype(
        jnp.bfloat16
    )
    both_local = jnp.concatenate((key_local, value_local), axis=-1).reshape(
        dialogs, shard_rows, 2 * model_width
    )
    both_window = with_halo(both_local, (("seq", 1),), HALO)
    key_rows = both_window[:, :, :model_width].reshape(dialogs, window, HEADS, head_dim)
    value_rows = both_window[:, :, model_width:].reshape(dialogs, window, HEADS, head_dim)
    group_pad = jnp.pad(group_ids, ((0, 0), (HALO, HALO)), constant_values=-10)
    key_group = lax.dynamic_slice_in_dim(group_pad, offset, window, 1)
    query_group = lax.dynamic_slice_in_dim(group_ids, offset, shard_rows, 1)
    query_pos = offset + jnp.arange(shard_rows, dtype=jnp.int32)
    key_pos = offset - HALO + jnp.arange(window, dtype=jnp.int32)
    allowed = build_allowed(query_group, query_pos, key_group, key_pos, lengths)
    scaling = head_dim ** (-0.5)
    scores = jnp.einsum("brhd,bwhd->bhrw", queries, key_rows, preferred_element_type=jnp.float32)
    scores = jnp.where(allowed[:, None], scores * scaling, NEGATIVE)
    row_max = jnp.max(scores, axis=-1, keepdims=True)
    exponent = jnp.exp(scores - row_max)
    probs = exponent / jnp.sum(exponent, axis=-1, keepdims=True)
    probs_low = probs.astype(jnp.bfloat16)
    student_mix = jnp.einsum(
        "bhrw,bwhd->brhd", probs_low, value_rows, preferred_element_type=jnp.float32
    ).astype(jnp.bfloat16)
    mix_flat = student_mix.reshape(dialogs * shard_rows, model_width)
    student_vel = jnp.dot(mix_flat, w_output, preferred_element_type=jnp.float32)
    query_valid = (query_pos[None, :] < lengths[:, None]).reshape(-1)
    difference = jnp.where(query_valid[:, None], student_vel - teacher_vel, 0.0)
    square_local = jnp.sum(difference * difference)
    count_local = jnp.sum(query_valid.astype(jnp.float32))
    grad_vel = difference.astype(jnp.bfloat16)
    grad_mix = jnp.dot(grad_vel, w_output.T, preferred_element_type=jnp.float32).astype(
        jnp.bfloat16
    )
    grad_mix = grad_mix.reshape(dialogs, shard_rows, HEADS, head_dim)
    grad_prob = jnp.einsum(
        "brhd,bwhd->bhrw", grad_mix, value_rows, preferred_element_type=jnp.float32
    )
    grad_score = probs * (grad_prob - jnp.sum(probs * grad_prob, axis=-1, keepdims=True)) * scaling
    grad_score = lax.optimization_barrier(grad_score)
    grad_key = split_product("bhrw,brhd->bwhd", grad_score, queries, True)
    grad_value = jnp.einsum(
        "bhrw,brhd->bwhd", probs_low, grad_mix, preferred_element_type=jnp.float32
    )
    grad_both = jnp.concatenate(
        (
            grad_key.reshape(dialogs, window, model_width),
            grad_value.reshape(dialogs, window, model_width),
        ),
        axis=-1,
    )
    by_head = grad_both.reshape(window, 2, HEADS, head_dim).transpose(0, 2, 1, 3)
    windows = lax.all_to_all(
        by_head.astype(jnp.bfloat16), "seq", split_axis=1, concat_axis=0, tiled=True
    )
    windows = windows.reshape(seq_count, window, 2 * head_dim).astype(jnp.float32)
    blank = jnp.zeros((1, HALO, 2 * head_dim), jnp.float32)
    from_prev = jnp.concatenate((blank, windows[:-1, HALO + shard_rows :]), axis=0)
    from_next = jnp.concatenate((windows[1:, :HALO], blank), axis=0)
    owned_rows = windows[:, HALO : HALO + shard_rows]
    if shard_rows >= 2 * HALO:
        middle = jnp.zeros((seq_count, shard_rows - 2 * HALO, 2 * head_dim), jnp.float32)
        owned_rows = owned_rows + jnp.concatenate((from_prev, middle, from_next), axis=1)
    else:
        owned_rows = owned_rows.at[:, :HALO].add(from_prev)
        owned_rows = owned_rows.at[:, shard_rows - HALO :].add(from_next)
    head_grads = owned_rows.reshape(frames, 2 * head_dim).astype(jnp.bfloat16)
    normed_all = doubling_gather(flat_rows, "seq", 0)
    partial = jnp.dot(normed_all.T, head_grads, preferred_element_type=jnp.float32)
    dp_count = lax.axis_size("dp")
    block = rows_each * 2 * head_dim
    partial = partial.reshape(dp_count * seq_count, block)
    lane = jnp.arange(2 * head_dim)
    scalars = jnp.where(lane == 0, square_local, jnp.where(lane == 1, count_local, 0.0))
    partial = jnp.concatenate(
        (partial, jnp.broadcast_to(scalars, (dp_count * seq_count, 2 * head_dim))), axis=1
    )
    mine = lax.all_to_all(partial, ("dp", "seq"), split_axis=0, concat_axis=0, tiled=True)
    mine = mine.reshape(dp_count, seq_count, block + 2 * head_dim)
    totals = mine[:, :, block:].sum((0, 1))
    square_sum, frame_count = totals[0], totals[1]
    mean_error = square_sum / (frame_count * model_width)
    mine = mine[:, :, :block].sum(0) * lax.rsqrt(frame_count)
    mine = mine.reshape(HEADS, rows_each, 2, head_dim).transpose(2, 1, 0, 3)
    grad_inputs = mine.reshape(2, rows_each, model_width)
    return (grad_inputs, mean_error)


def solution(mesh):
    in_specs = (
        P("dp", "seq", None),
        P("dp", "seq", None),
        P("dp"),
        P("dp", None),
        P("dp"),
        P(),
        P(),
        P(),
        P(None, ("dp", "seq"), None),
        P(("dp", "seq"), None),
    )
    out_specs = (P(None, ("dp", "seq"), None), P())
    return jax.shard_map(shards, mesh=mesh, in_specs=in_specs, out_specs=out_specs, check_vma=False)
```
